512 devices in a mesh: box: 512 (over y, x, z, core).
Axes of the slice: x: 4, y: 8, z: 8, core: 2. Of those that a mesh axis runs over, the one named last changes fastest.
Arguments:
- positions: float32 [3, 131072], P(None, 'box'), may hold values from -1 to 1
- leaf_centers: float32 [3, 2048], P(None, 'box'), may hold values from -1 to 1
- atom_counts: int32 [2048], P('box'), may hold values from 32 to 64
- features: bfloat16 [131072, 128], P('box'), may hold values from -6 to 6
- msg_weight: bfloat16 [128, 128], replicated, may hold values from -0.5 to 0.5
- trans_weight: float32 [35, 35], replicated, may hold values from -0.03125 to 0.03125
- read_weight: float32 [128], replicated, may hold values from -0.5 to 0.5
- pair_target: int32 [55296], P('box'), may hold values from 0 to 3
- pair_source: int32 [55296], P('box'), may hold values from 0 to 11
- pair_live: int32 [55296], P('box'), may hold values 0 or 1
- far_list: int32 [64, 32], replicated, may hold values from 0 to 63, as said below
Outputs:
- atom_energy: float32 [131072], P('box')
- forces: float32 [3, 131072], P(None, 'box')
- grad_msg: float32 [128, 128], replicated
- grad_trans: float32 [35, 35], replicated
- grad_read: float32 [128], replicated
The draws below stay inside these ranges and needn't reach their ends.
Inputs may be any that keep to these rules, and one draw needn't show every extreme that they name: `far_list`: each row names 32 different level-two boxes, none of them the row's own box.
All inputs are finite; a program needn't handle non-finite values. No bound on the sum of `pair_live` on one device may be relied on, other than what follows from the above.
Results may differ from the reference program's by a relative error of at most 0.0047.
Values may be sent and summed in bfloat16 or wider, within the bound.
No kernel may reach another device: no remote copies, remote signals or barrier semaphores. Data moves between devices by JAX's collectives and lax.ppermute only.
A program may use at most 64 MiB of HBM per device.

```python
import jax
import jax.numpy as jnp
from jax import lax

C = 128
NTERM = 35
LEAF_ATOMS = 64
PAIR_LEAF = 27
LEAF_DEV = 4
LEAVES = 2048
ATOMS = 131072
PAIRS = 55296
GROUPS = 64
LIST = 32
N_BOX = 512


def draw_far_list(key, part):
    row_keys = jax.random.split(jax.random.fold_in(key, 17), GROUPS)
    shuffled = jax.vmap(lambda row_key: jax.random.permutation(row_key, GROUPS - 1))(row_keys)[:, :LIST]
    own_box = jnp.arange(GROUPS, dtype=jnp.int32)[:, None]
    shuffled = shuffled.astype(jnp.int32)
    return jnp.where(shuffled >= own_box, shuffled + 1, shuffled).astype(jnp.int32)


def plant(drawn, rng, smallest, high):
    longest = drawn.shape.index(max(drawn.shape))
    spots = []
    for shift in (0, 1):
        where = [jax.random.randint(jax.random.fold_in(rng, axis), (), 0, length) for axis, length in enumerate(drawn.shape)]
        where[longest] = (where[longest] + shift) % drawn.shape[longest]
        spots.append(tuple(where))
    return drawn.at[spots[0]].set(smallest).at[spots[1]].set(high)


def block_levels(key, dims, pieces, low, high):
    level, own = 1.0, jax.random.fold_in(key, 6)
    for axis_at, blocks in pieces:
        heights = jnp.exp(jax.random.uniform(jax.random.fold_in(own, axis_at), (blocks,), jnp.float32, low / len(pieces), high / len(pieces)))
        level = level * jnp.repeat(heights, dims[axis_at] // blocks).reshape([-1 if axis == axis_at else 1 for axis in range(len(dims))])
    return level


def centred(rng, extent, width, bound, pieces=(), held_as=jnp.bfloat16):
    drawn = jax.random.normal(rng, extent, jnp.float32) * width
    if len(pieces) > 0:
        drawn = block_levels(rng, extent, pieces, -0.22, 0.18) * drawn
    return jnp.clip(drawn, min=-bound, max=bound).astype(held_as)


def setup_inputs(seed: int = 0) -> dict:
    keys = jax.random.split(jax.random.key(seed), 12)
    positions = jnp.clip(jax.random.uniform(keys[0], (3, ATOMS), jnp.float32, -1.0, 1.0) * block_levels(keys[0], (3, ATOMS), ((1, 512),), -0.4, 0.0), -1.0, 1.0)
    leaf_centers = jnp.clip(jax.random.uniform(keys[1], (3, LEAVES), jnp.float32, -1.0, 1.0) * block_levels(keys[1], (3, LEAVES), ((1, 512),), -0.4, 0.0), -1.0, 1.0)
    atom_counts = plant(jax.random.randint(keys[2], (LEAVES,), LEAF_ATOMS // 2, LEAF_ATOMS + 1), jax.random.fold_in(keys[2], 1), LEAF_ATOMS // 2, LEAF_ATOMS).astype(jnp.int32)
    features = centred(keys[3], (ATOMS, C), 1.0, 6.0, ((0, 512),))
    msg_weight = centred(keys[4], (C, C), C ** -0.5, 0.5)
    trans_weight = centred(keys[5], (NTERM, NTERM), (NTERM * LIST * LEAF_DEV * LEAF_ATOMS // 8) ** -0.5, 0.03125, (), jnp.float32)
    read_weight = centred(keys[6], (C,), C ** -0.5, 0.5, (), jnp.float32)
    pair_target = plant(jax.random.randint(keys[7], (PAIRS,), 0, LEAF_DEV), jax.random.fold_in(keys[7], 1), 0, LEAF_DEV - 1).astype(jnp.int32)
    pair_source = plant(jax.random.randint(keys[8], (PAIRS,), 0, 3 * LEAF_DEV), jax.random.fold_in(keys[8], 1), 0, (3 * LEAF_DEV) - 1).astype(jnp.int32)
    pair_live = plant((jax.random.randint(keys[9], (PAIRS,), 0, 4) < 3).astype(jnp.int32), jax.random.fold_in(keys[9], 1), 0, 1)
    far_list = draw_far_list(jax.random.fold_in(keys[11], 71), 0)
    return dict(positions=positions, leaf_centers=leaf_centers, atom_counts=atom_counts, features=features, msg_weight=msg_weight, trans_weight=trans_weight, read_weight=read_weight, pair_target=pair_target, pair_source=pair_source, pair_live=pair_live, far_list=far_list)


PRECISE = lax.Precision.HIGHEST
GAMMA = 3.0
NEAR_SCALE = 0.3
REL_SCALE = 0.5
EXPONENTS = [(power_x, power_y, degree - power_x - power_y) for degree in range(5) for power_x in range(degree, -1, -1) for power_y in range(degree - power_x, -1, -1)]

def monomials(relative):
    powers = []
    for axis_id in range(3):
        coords = relative[axis_id]
        stacked = [jnp.ones_like(coords), coords]
        for degree in range(2, 5):
            stacked.append(stacked[-1] * coords)
        powers.append(stacked)
    return jnp.stack([powers[0][ex_a] * powers[1][ex_b] * powers[2][ex_c] for ex_a, ex_b, ex_c in EXPONENTS])

def near_field(pos_own, pos_ext, hid_ext, targets, sources, alive):
    leaves = pos_own.shape[1] // LEAF_ATOMS
    channels = hid_ext.shape[0]
    own_leaf = pos_own.reshape(3, leaves, LEAF_ATOMS)
    ext_leaf = pos_ext.reshape(3, 3 * leaves, LEAF_ATOMS)
    feat_leaf = hid_ext.reshape(channels, 3 * leaves, LEAF_ATOMS)
    leaf_ids = jnp.arange(leaves, dtype=jnp.int32)
    blocks = (targets.reshape(-1, PAIR_LEAF), sources.reshape(-1, PAIR_LEAF), alive.reshape(-1, PAIR_LEAF))

    def one_block(accumulated, pair_block):
        tgt_ids, src_ids, live_ids = pair_block
        near_pos = own_leaf[:, tgt_ids]
        far_pos = ext_leaf[:, src_ids]
        dist_sq = jnp.zeros((tgt_ids.shape[0], LEAF_ATOMS, LEAF_ATOMS), jnp.float32)
        for axis_id in range(3):
            offset_ax = near_pos[axis_id][:, :, None] - far_pos[axis_id][:, None, :]
            dist_sq = dist_sq + offset_ax * offset_ax
        kernel = (NEAR_SCALE * jnp.exp(-GAMMA * dist_sq) * live_ids.astype(jnp.float32)[:, None, None]).astype(jnp.bfloat16)
        source_feat = feat_leaf[:, src_ids].astype(jnp.bfloat16)
        contrib = jnp.einsum('pij,cpj->pic', kernel.astype(jnp.float32), source_feat.astype(jnp.float32), precision=PRECISE)
        onehot = (tgt_ids[None, :] == leaf_ids[:, None]).astype(jnp.float32)
        return (accumulated + jnp.einsum('tp,pic->tic', onehot, contrib, precision=PRECISE), None)
    initial = jnp.zeros((leaves, LEAF_ATOMS, channels), jnp.float32)
    accumulated, unused = lax.scan(jax.checkpoint(one_block), initial, blocks)
    return accumulated.reshape(leaves * LEAF_ATOMS, channels)

def energies(positions, hidden, trans_weight, read_weight, leaf_centers, mask_f, pair_target, pair_source, pair_live, far_list):
    atom_num = LEAF_DEV * LEAF_ATOMS
    pair_num = PAIR_LEAF * LEAF_DEV
    hidden_t = (hidden * mask_f[:, None]).T
    pos_pad = jnp.pad(positions, ((0, 0), (atom_num, atom_num)))
    hid_pad = jnp.pad(hidden_t, ((0, 0), (atom_num, atom_num)))

    def per_device(index):
        start_at = index * atom_num
        own = lax.dynamic_slice_in_dim(positions, start_at, atom_num, 1)
        ext = lax.dynamic_slice_in_dim(pos_pad, start_at, 3 * atom_num, 1)
        feat_ext = lax.dynamic_slice_in_dim(hid_pad, start_at, 3 * atom_num, 1)
        pair_at = index * pair_num
        tgt_ids = lax.dynamic_slice_in_dim(pair_target, pair_at, pair_num, 0)
        src_ids = lax.dynamic_slice_in_dim(pair_source, pair_at, pair_num, 0)
        live_ids = lax.dynamic_slice_in_dim(pair_live, pair_at, pair_num, 0)
        return near_field(own, ext, feat_ext, tgt_ids, src_ids, live_ids)
    near_val = lax.map(jax.checkpoint(per_device), jnp.arange(N_BOX, dtype=jnp.int32))
    centers = jnp.repeat(leaf_centers, LEAF_ATOMS, axis=1)
    basis_val = monomials((positions - centers) * REL_SCALE)
    basis_dev = basis_val.reshape(NTERM, N_BOX, atom_num)
    hid_dev = hidden_t.reshape(C, N_BOX, atom_num)
    moments = jnp.einsum('kda,cda->dkc', basis_dev, hid_dev, precision=PRECISE)
    group_moment = lax.optimization_barrier(jnp.sum(moments.reshape(GROUPS, 8, NTERM, C), axis=1))
    counts_mat = lax.optimization_barrier(jnp.sum((far_list[:, :, None] == jnp.arange(GROUPS, dtype=jnp.int32)[None, None, :]).astype(jnp.float32), axis=1))
    gathered = jnp.einsum('bj,jkc->bkc', counts_mat, group_moment, precision=PRECISE)
    local_exp = jnp.einsum('kq,bqc->bkc', trans_weight, gathered, precision=PRECISE)
    local_dev = jnp.repeat(local_exp, 8, axis=0)
    potential = jnp.einsum('kda,dkc->dac', basis_dev, local_dev, precision=PRECISE)
    pre_act = near_val + potential
    activ = pre_act * jax.nn.sigmoid(pre_act)
    energy = jnp.einsum('dac,c->da', activ, read_weight, precision=PRECISE).reshape(ATOMS)
    return mask_f * energy

def reference(positions, leaf_centers, atom_counts, features, msg_weight, trans_weight, read_weight, pair_target, pair_source, pair_live, far_list):
    slot_ids = jnp.arange(LEAF_ATOMS, dtype=jnp.int32)
    mask_f = (slot_ids[None, :] < atom_counts[:, None]).astype(jnp.float32).reshape(ATOMS)
    hidden = jnp.dot(features, msg_weight, preferred_element_type=jnp.float32)

    def total_fn(pos_arg, hid_arg, trans_arg, read_arg):
        return energies(pos_arg, hid_arg, trans_arg, read_arg, leaf_centers, mask_f, pair_target, pair_source, pair_live, far_list)
    atom_energy, pullback = jax.vjp(total_fn, positions, hidden, trans_weight, read_weight)
    d_pos, d_hidden, grad_trans, grad_read = pullback(jnp.ones_like(atom_energy))
    grad_msg = jnp.dot(features.astype(jnp.float32).T, d_hidden, precision=PRECISE)
    return (atom_energy, -d_pos, grad_msg, grad_trans, grad_read)
```

```python
import jax
import jax.numpy as jnp
from jax import lax
from jax.sharding import Mesh, PartitionSpec as P

LEAF_ATOMS = 64
PAIR_LEAF = 27
BOX = ("grp", "sub")


PRECISE = lax.Precision.HIGHEST
GAMMA = 3.0
NEAR_SCALE = 0.3
REL_SCALE = 0.5
EXPONENTS = [
    (power_x, power_y, degree - power_x - power_y)
    for degree in range(5)
    for power_x in range(degree, -1, -1)
    for power_y in range(degree - power_x, -1, -1)
]


def extended(block, sides, width):
    for axis, dim in sides:
        count = lax.axis_size(axis)
        forward = [(i, i + 1) for i in range(count - 1)]
        backward = [(target, source) for source, target in forward]
        low = lax.ppermute(
            lax.slice_in_dim(block, block.shape[dim] - width, None, axis=dim), axis, forward
        )
        high = lax.ppermute(lax.slice_in_dim(block, 0, width, axis=dim), axis, backward)
        block = jnp.concatenate([low, block, high], axis=dim)
    return block


def passed_along(block, axis, distance):
    devices = range(lax.axis_size(axis))
    route = [(i - distance, i) for i in devices if i - distance in devices]
    return lax.ppermute(block, axis, route)


def monomials(relative):
    powers = []
    for axis_id in range(3):
        coords = relative[axis_id]
        stacked = [jnp.ones_like(coords), coords]
        for degree in range(2, 5):
            stacked.append(stacked[-1] * coords)
        powers.append(stacked)
    return jnp.stack(
        [powers[0][ex_a] * powers[1][ex_b] * powers[2][ex_c] for ex_a, ex_b, ex_c in EXPONENTS]
    )


def near_field(pos_own, pos_ext, hid_ext, targets, sources, alive):
    leaves = pos_own.shape[1] // LEAF_ATOMS
    channels = hid_ext.shape[0]
    own_leaf = pos_own.reshape(3, leaves, LEAF_ATOMS)
    ext_leaf = pos_ext.reshape(3, 3 * leaves, LEAF_ATOMS)
    feat_leaf = hid_ext.reshape(channels, 3 * leaves, LEAF_ATOMS)
    leaf_ids = jnp.arange(leaves, dtype=jnp.int32)
    blocks = (
        targets.reshape(-1, PAIR_LEAF),
        sources.reshape(-1, PAIR_LEAF),
        alive.reshape(-1, PAIR_LEAF),
    )

    def one_block(accumulated, pair_block):
        tgt_ids, src_ids, live_ids = pair_block
        near_pos = own_leaf[:, tgt_ids]
        far_pos = ext_leaf[:, src_ids]
        dist_sq = jnp.zeros((tgt_ids.shape[0], LEAF_ATOMS, LEAF_ATOMS), jnp.float32)
        for axis_id in range(3):
            offset_ax = near_pos[axis_id][:, :, None] - far_pos[axis_id][:, None, :]
            dist_sq = dist_sq + offset_ax * offset_ax
        kernel = (
            NEAR_SCALE * jnp.exp(-GAMMA * dist_sq) * live_ids.astype(jnp.float32)[:, None, None]
        ).astype(jnp.bfloat16)
        source_feat = feat_leaf[:, src_ids].astype(jnp.bfloat16)
        contrib = jnp.einsum(
            "pij,cpj->pic", kernel, source_feat, preferred_element_type=jnp.float32
        )
        onehot = (tgt_ids[None, :] == leaf_ids[:, None]).astype(jnp.float32)
        return (accumulated + jnp.einsum("tp,pic->tic", onehot, contrib, precision=PRECISE), None)

    initial = jnp.zeros((leaves, LEAF_ATOMS, channels), jnp.float32)
    accumulated, unused = lax.scan(jax.checkpoint(one_block), initial, blocks)
    return accumulated.reshape(leaves * LEAF_ATOMS, channels)


def on_device(
    positions,
    leaf_centers,
    atom_counts,
    features,
    msg_weight,
    trans_weight,
    read_weight,
    pair_target,
    pair_source,
    pair_live,
    far_list,
):
    atom_num = positions.shape[1]
    groups = lax.axis_size("grp")
    group_id = lax.axis_index("grp")
    slot_ids = jnp.arange(LEAF_ATOMS, dtype=jnp.int32)
    mask_f = (slot_ids[None, :] < atom_counts[:, None]).astype(jnp.float32).reshape(atom_num)
    hidden_t = (
        jnp.einsum("ic,ai->ca", msg_weight, features, preferred_element_type=jnp.float32)
        * mask_f[None, :]
    )
    pos_ext = extended(positions, ((BOX, 1),), atom_num)
    hid_ext = extended(hidden_t.astype(jnp.bfloat16), ((BOX, 1),), atom_num).astype(jnp.float32)

    def near_part(own, ext, feat_ext):
        return near_field(own, ext, feat_ext, pair_target, pair_source, pair_live)

    near_val, near_back = jax.vjp(near_part, positions, pos_ext, hid_ext)
    centers = jnp.repeat(leaf_centers, LEAF_ATOMS, axis=1)

    def far_basis(coords):
        return monomials((coords - centers) * REL_SCALE)

    basis_val, basis_back = jax.vjp(far_basis, positions)
    moment = jnp.einsum("ka,ca->kc", basis_val, hidden_t, precision=PRECISE)
    counts_mat = jnp.sum(
        (far_list[:, :, None] == jnp.arange(groups, dtype=jnp.int32)[None, None, :]).astype(
            jnp.float32
        ),
        axis=1,
    )
    row_weights = lax.dynamic_index_in_dim(counts_mat, group_id, 0, keepdims=False)
    col_weights = lax.dynamic_index_in_dim(counts_mat, group_id, 1, keepdims=False)
    moment_part = lax.psum_scatter(moment, "sub", scatter_dimension=1, tiled=True)
    moment_tab = lax.all_gather(moment_part, "grp", axis=0)
    gathered_part = jnp.einsum("j,jkc->kc", row_weights, moment_tab, precision=PRECISE)
    local_part = jnp.dot(trans_weight, gathered_part, precision=PRECISE)
    local_exp = lax.all_gather(local_part, "sub", axis=1, tiled=True)
    potential = jnp.einsum("ka,kc->ac", basis_val, local_exp, precision=PRECISE)
    pre_act = near_val + potential
    sigma = jax.nn.sigmoid(pre_act)
    activ = pre_act * sigma
    atom_energy = mask_f * jnp.dot(activ, read_weight, precision=PRECISE)
    d_pre = mask_f[:, None] * read_weight[None, :] * (sigma + pre_act * sigma * (1.0 - sigma))
    grad_read_part = jnp.dot(mask_f, activ, precision=PRECISE)
    d_local = jnp.dot(basis_val, d_pre, precision=PRECISE)
    d_basis = jnp.einsum("kc,ac->ka", local_exp, d_pre, precision=PRECISE)
    d_local_part = lax.psum_scatter(d_local, "sub", scatter_dimension=1, tiled=True)
    grad_trans_part = jnp.einsum("kc,qc->kq", d_local_part, gathered_part, precision=PRECISE)
    d_gathered_part = jnp.dot(trans_weight.T, d_local_part, precision=PRECISE)
    d_tab = lax.all_gather(d_gathered_part, "grp", axis=0)
    d_moment_part = jnp.einsum("b,bkc->kc", col_weights, d_tab, precision=PRECISE)
    d_moment = lax.all_gather(d_moment_part, "sub", axis=1, tiled=True)
    d_basis = d_basis + jnp.dot(d_moment, hidden_t, precision=PRECISE)
    d_hidden_far = jnp.einsum("ka,kc->ca", basis_val, d_moment, precision=PRECISE)
    (d_far_pos,) = basis_back(d_basis)
    d_own, d_ext, d_feat_ext = near_back(d_pre)
    low_pos, low_feat = passed_along((d_ext[:, :atom_num], d_feat_ext[:, :atom_num]), BOX, -1)
    high_pos, high_feat = (
        passed_along(d_ext[:, 2 * atom_num :].astype(jnp.bfloat16), BOX, 1).astype(jnp.float32),
        passed_along(d_feat_ext[:, 2 * atom_num :].astype(jnp.bfloat16), BOX, 1).astype(
            jnp.float32
        ),
    )
    d_hidden_t = (
        d_feat_ext[:, atom_num : 2 * atom_num] + low_feat + high_feat + d_hidden_far
    ) * mask_f[None, :]
    grad_msg_part = jnp.einsum(
        "ai,ca->ic", features.astype(jnp.float32), d_hidden_t, precision=PRECISE
    )
    grad_msg, grad_trans, grad_read = lax.psum(
        (grad_msg_part, grad_trans_part, grad_read_part), BOX
    )
    forces = -(d_own + d_ext[:, atom_num : 2 * atom_num] + low_pos + high_pos + d_far_pos)
    return (atom_energy, forces, grad_msg, grad_trans, grad_read)


def solution(mesh):
    split = Mesh(mesh.devices.reshape(-1, 8), ("grp", "sub"))
    return jax.shard_map(
        on_device,
        mesh=split,
        in_specs=(
            P(None, BOX),
            P(None, BOX),
            P(BOX),
            P(BOX, None),
            P(),
            P(),
            P(),
            P(BOX),
            P(BOX),
            P(BOX),
            P(),
        ),
        out_specs=(P(BOX), P(None, BOX), P(), P(), P()),
        check_vma=False,
    )
```

```python
import jax
import jax.numpy as jnp
from jax import lax
from jax.sharding import PartitionSpec as P

LEAF_ATOMS = 64
PAIR_LEAF = 27


PRECISE = lax.Precision.HIGHEST
GAMMA = 3.0
NEAR_SCALE = 0.3
REL_SCALE = 0.5
EXPONENTS = [
    (power_x, power_y, degree - power_x - power_y)
    for degree in range(5)
    for power_x in range(degree, -1, -1)
    for power_y in range(degree - power_x, -1, -1)
]


def extended(block, sides, width):
    for axis, dim in sides:
        count = lax.axis_size(axis)
        forward = [(i, i + 1) for i in range(count - 1)]
        backward = [(target, source) for source, target in forward]
        low = lax.ppermute(
            lax.slice_in_dim(block, block.shape[dim] - width, None, axis=dim), axis, forward
        )
        high = lax.ppermute(lax.slice_in_dim(block, 0, width, axis=dim), axis, backward)
        block = jnp.concatenate([low, block, high], axis=dim)
    return block


def passed_along(block, axis, distance):
    devices = range(lax.axis_size(axis))
    route = [(i - distance, i) for i in devices if i - distance in devices]
    return lax.ppermute(block, axis, route)


def monomials(relative):
    powers = []
    for axis_id in range(3):
        coords = relative[axis_id]
        stacked = [jnp.ones_like(coords), coords]
        for degree in range(2, 5):
            stacked.append(stacked[-1] * coords)
        powers.append(stacked)
    return jnp.stack(
        [powers[0][ex_a] * powers[1][ex_b] * powers[2][ex_c] for ex_a, ex_b, ex_c in EXPONENTS]
    )


def near_field(pos_own, pos_ext, hid_ext, targets, sources, alive):
    leaves = pos_own.shape[1] // LEAF_ATOMS
    channels = hid_ext.shape[0]
    own_leaf = pos_own.reshape(3, leaves, LEAF_ATOMS)
    ext_leaf = pos_ext.reshape(3, 3 * leaves, LEAF_ATOMS)
    feat_leaf = hid_ext.reshape(channels, 3 * leaves, LEAF_ATOMS)
    leaf_ids = jnp.arange(leaves, dtype=jnp.int32)
    blocks = (
        targets.reshape(-1, PAIR_LEAF),
        sources.reshape(-1, PAIR_LEAF),
        alive.reshape(-1, PAIR_LEAF),
    )

    def one_block(accumulated, pair_block):
        tgt_ids, src_ids, live_ids = pair_block
        near_pos = own_leaf[:, tgt_ids]
        far_pos = ext_leaf[:, src_ids]
        dist_sq = jnp.zeros((tgt_ids.shape[0], LEAF_ATOMS, LEAF_ATOMS), jnp.float32)
        for axis_id in range(3):
            offset_ax = near_pos[axis_id][:, :, None] - far_pos[axis_id][:, None, :]
            dist_sq = dist_sq + offset_ax * offset_ax
        kernel = (
            NEAR_SCALE * jnp.exp(-GAMMA * dist_sq) * live_ids.astype(jnp.float32)[:, None, None]
        ).astype(jnp.bfloat16)
        source_feat = feat_leaf[:, src_ids].astype(jnp.bfloat16)
        contrib = jnp.einsum(
            "pij,cpj->pic", kernel, source_feat, preferred_element_type=jnp.float32
        )
        onehot = (tgt_ids[None, :] == leaf_ids[:, None]).astype(jnp.float32)
        return (accumulated + jnp.einsum("tp,pic->tic", onehot, contrib, precision=PRECISE), None)

    initial = jnp.zeros((leaves, LEAF_ATOMS, channels), jnp.float32)
    accumulated, unused = lax.scan(jax.checkpoint(one_block), initial, blocks)
    return accumulated.reshape(leaves * LEAF_ATOMS, channels)


def xor_swap(block, bit):
    count = lax.axis_size("box")
    return lax.ppermute(block, "box", [(i, i ^ (1 << bit)) for i in range(count)])


def tree_sum(block, bits):
    for bit in bits:
        block = block + xor_swap(block, bit)
    return block


def split_sum(block, index, bits):
    for bit in bits:
        half = block.shape[1] // 2
        lower, upper = block[:, :half], block[:, half:]
        up = ((index >> bit) & 1) == 1
        keep = jnp.where(up, upper, lower)
        send = jnp.where(up, lower, upper)
        block = keep + xor_swap(send, bit)
    return block


def tree_gather(block, index, bits, axis):
    for bit in bits:
        other = xor_swap(block, bit)
        up = ((index >> bit) & 1) == 1
        block = jnp.where(
            up,
            jnp.concatenate([other, block], axis=axis),
            jnp.concatenate([block, other], axis=axis),
        )
    return block


def on_device(
    positions,
    leaf_centers,
    atom_counts,
    features,
    msg_weight,
    trans_weight,
    read_weight,
    pair_target,
    pair_source,
    pair_live,
    far_list,
):
    atom_num = positions.shape[1]
    all_bits = lax.axis_size("box").bit_length() - 1
    sub_bits = tuple(range(3))
    grp_bits = tuple(range(3, all_bits))
    index = lax.axis_index("box")
    groups = lax.axis_size("box") // 8
    group_id = index // 8
    slot_ids = jnp.arange(LEAF_ATOMS, dtype=jnp.int32)
    mask_f = (slot_ids[None, :] < atom_counts[:, None]).astype(jnp.float32).reshape(atom_num)
    hidden_t = (
        jnp.einsum("ic,ai->ca", msg_weight, features, preferred_element_type=jnp.float32)
        * mask_f[None, :]
    )
    pos_ext = extended(positions, (("box", 1),), atom_num)
    hid_ext = extended(hidden_t.astype(jnp.bfloat16), (("box", 1),), atom_num).astype(jnp.float32)

    def near_part(own, ext, feat_ext):
        return near_field(own, ext, feat_ext, pair_target, pair_source, pair_live)

    near_val, near_back = jax.vjp(near_part, positions, pos_ext, hid_ext)
    centers = jnp.repeat(leaf_centers, LEAF_ATOMS, axis=1)

    def far_basis(coords):
        return monomials((coords - centers) * REL_SCALE)

    basis_val, basis_back = jax.vjp(far_basis, positions)
    moment = jnp.einsum("ka,ca->kc", basis_val, hidden_t, precision=PRECISE)
    counts_mat = jnp.sum(
        (far_list[:, :, None] == jnp.arange(groups, dtype=jnp.int32)[None, None, :]).astype(
            jnp.float32
        ),
        axis=1,
    )
    row_weights = lax.dynamic_index_in_dim(counts_mat, group_id, 0, keepdims=False)
    col_weights = lax.dynamic_index_in_dim(counts_mat, group_id, 1, keepdims=False)
    moment_part = split_sum(moment, index, sub_bits[::-1])
    moment_tab = tree_gather(moment_part[None], index, grp_bits, 0)
    gathered_part = jnp.einsum("j,jkc->kc", row_weights, moment_tab, precision=PRECISE)
    local_part = jnp.dot(trans_weight, gathered_part, precision=PRECISE)
    local_exp = tree_gather(local_part, index, sub_bits, 1)
    potential = jnp.einsum("ka,kc->ac", basis_val, local_exp, precision=PRECISE)
    pre_act = near_val + potential
    sigma = jax.nn.sigmoid(pre_act)
    activ = pre_act * sigma
    atom_energy = mask_f * jnp.dot(activ, read_weight, precision=PRECISE)
    d_pre = mask_f[:, None] * read_weight[None, :] * (sigma + pre_act * sigma * (1.0 - sigma))
    grad_read_part = jnp.dot(mask_f, activ, precision=PRECISE)
    d_local = jnp.dot(basis_val, d_pre, precision=PRECISE)
    d_basis = jnp.einsum("kc,ac->ka", local_exp, d_pre, precision=PRECISE)
    d_local_part = split_sum(d_local, index, sub_bits[::-1])
    grad_trans_part = jnp.einsum("kc,qc->kq", d_local_part, gathered_part, precision=PRECISE)
    d_gathered_part = jnp.dot(trans_weight.T, d_local_part, precision=PRECISE)
    d_tab = tree_gather(d_gathered_part[None], index, grp_bits, 0)
    d_moment_part = jnp.einsum("b,bkc->kc", col_weights, d_tab, precision=PRECISE)
    d_moment = tree_gather(d_moment_part, index, sub_bits, 1)
    d_basis = d_basis + jnp.dot(d_moment, hidden_t, precision=PRECISE)
    d_hidden_far = jnp.einsum("ka,kc->ca", basis_val, d_moment, precision=PRECISE)
    (d_far_pos,) = basis_back(d_basis)
    d_own, d_ext, d_feat_ext = near_back(d_pre)
    low_pos, low_feat = passed_along((d_ext[:, :atom_num], d_feat_ext[:, :atom_num]), "box", -1)
    high_pos, high_feat = (
        passed_along(d_ext[:, 2 * atom_num :].astype(jnp.bfloat16), "box", 1).astype(jnp.float32),
        passed_along(d_feat_ext[:, 2 * atom_num :].astype(jnp.bfloat16), "box", 1).astype(
            jnp.float32
        ),
    )
    d_hidden_t = (
        d_feat_ext[:, atom_num : 2 * atom_num] + low_feat + high_feat + d_hidden_far
    ) * mask_f[None, :]
    grad_msg_part = jnp.einsum(
        "ai,ca->ic", features.astype(jnp.float32), d_hidden_t, precision=PRECISE
    )
    flat = jnp.concatenate(
        [grad_msg_part.reshape(-1), grad_trans_part.reshape(-1), grad_read_part.reshape(-1)]
    )
    flat = tree_sum(flat, tuple(range(all_bits)))
    msg_size, trans_size = grad_msg_part.size, grad_trans_part.size
    grad_msg = flat[:msg_size].reshape(grad_msg_part.shape)
    grad_trans = flat[msg_size : msg_size + trans_size].reshape(grad_trans_part.shape)
    grad_read = flat[msg_size + trans_size :]
    forces = -(d_own + d_ext[:, atom_num : 2 * atom_num] + low_pos + high_pos + d_far_pos)
    return (atom_energy, forces, grad_msg, grad_trans, grad_read)


def solution(mesh):
    return jax.shard_map(
        on_device,
        mesh=mesh,
        in_specs=(
            P(None, "box"),
            P(None, "box"),
            P("box"),
            P("box", None),
            P(),
            P(),
            P(),
            P("box"),
            P("box"),
            P("box"),
            P(),
        ),
        out_specs=(P("box"), P(None, "box"), P(), P(), P()),
        check_vma=False,
    )
```

```python
import jax
import jax.numpy as jnp
from jax import lax
from jax.sharding import PartitionSpec as P

LEAF_ATOMS = 64
PAIR_LEAF = 27


PRECISE = lax.Precision.HIGHEST
GAMMA = 3.0
NEAR_SCALE = 0.3
REL_SCALE = 0.5
EXPONENTS = [
    (power_x, power_y, degree - power_x - power_y)
    for degree in range(5)
    for power_x in range(degree, -1, -1)
    for power_y in range(degree - power_x, -1, -1)
]


def extended(block, sides, width):
    for axis, dim in sides:
        count = lax.axis_size(axis)
        forward = [(i, i + 1) for i in range(count - 1)]
        backward = [(target, source) for source, target in forward]
        low = lax.ppermute(
            lax.slice_in_dim(block, block.shape[dim] - width, None, axis=dim), axis, forward
        )
        high = lax.ppermute(lax.slice_in_dim(block, 0, width, axis=dim), axis, backward)
        block = jnp.concatenate([low, block, high], axis=dim)
    return block


def passed_along(block, axis, distance):
    devices = range(lax.axis_size(axis))
    route = [(i - distance, i) for i in devices if i - distance in devices]
    return lax.ppermute(block, axis, route)


def monomials(relative):
    powers = []
    for axis_id in range(3):
        coords = relative[axis_id]
        stacked = [jnp.ones_like(coords), coords]
        for degree in range(2, 5):
            stacked.append(stacked[-1] * coords)
        powers.append(stacked)
    return jnp.stack(
        [powers[0][ex_a] * powers[1][ex_b] * powers[2][ex_c] for ex_a, ex_b, ex_c in EXPONENTS]
    )


def near_field(pos_own, pos_ext, hid_ext, targets, sources, alive):
    leaves = pos_own.shape[1] // LEAF_ATOMS
    channels = hid_ext.shape[0]
    own_leaf = pos_own.reshape(3, leaves, LEAF_ATOMS)
    ext_leaf = pos_ext.reshape(3, 3 * leaves, LEAF_ATOMS)
    feat_leaf = hid_ext.reshape(channels, 3 * leaves, LEAF_ATOMS)
    leaf_ids = jnp.arange(leaves, dtype=jnp.int32)
    blocks = (
        targets.reshape(-1, PAIR_LEAF),
        sources.reshape(-1, PAIR_LEAF),
        alive.reshape(-1, PAIR_LEAF),
    )

    def one_block(accumulated, pair_block):
        tgt_ids, src_ids, live_ids = pair_block
        near_pos = own_leaf[:, tgt_ids]
        far_pos = ext_leaf[:, src_ids]
        dist_sq = jnp.zeros((tgt_ids.shape[0], LEAF_ATOMS, LEAF_ATOMS), jnp.float32)
        for axis_id in range(3):
            offset_ax = near_pos[axis_id][:, :, None] - far_pos[axis_id][:, None, :]
            dist_sq = dist_sq + offset_ax * offset_ax
        kernel = (
            NEAR_SCALE * jnp.exp(-GAMMA * dist_sq) * live_ids.astype(jnp.float32)[:, None, None]
        ).astype(jnp.bfloat16)
        source_feat = feat_leaf[:, src_ids].astype(jnp.bfloat16)
        contrib = jnp.einsum(
            "pij,cpj->pic", kernel, source_feat, preferred_element_type=jnp.float32
        )
        onehot = (tgt_ids[None, :] == leaf_ids[:, None]).astype(jnp.float32)
        return (accumulated + jnp.einsum("tp,pic->tic", onehot, contrib, precision=PRECISE), None)

    initial = jnp.zeros((leaves, LEAF_ATOMS, channels), jnp.float32)
    accumulated, unused = lax.scan(jax.checkpoint(one_block), initial, blocks)
    return accumulated.reshape(leaves * LEAF_ATOMS, channels)


def xor_swap(block, bit):
    count = lax.axis_size("box")
    return lax.ppermute(block, "box", [(i, i ^ (1 << bit)) for i in range(count)])


def tree_sum(block, bits):
    for bit in bits:
        block = block + xor_swap(block, bit)
    return block


def split_sum(block, index, bits):
    for bit in bits:
        half = block.shape[-1] // 2
        lower, upper = block[..., :half], block[..., half:]
        up = ((index >> bit) & 1) == 1
        keep = jnp.where(up, upper, lower)
        send = jnp.where(up, lower, upper)
        block = keep + xor_swap(send, bit)
    return block


def tree_gather_sum(block, extra, index, bits, axis):
    for bit in bits:
        other, other_extra = xor_swap((block, extra), bit)
        up = ((index >> bit) & 1) == 1
        block = jnp.where(
            up,
            jnp.concatenate([other, block], axis=axis),
            jnp.concatenate([block, other], axis=axis),
        )
        extra = extra + other_extra
    return block, extra


def tree_gather(block, index, bits, axis):
    for bit in bits:
        other = xor_swap(block, bit)
        up = ((index >> bit) & 1) == 1
        block = jnp.where(
            up,
            jnp.concatenate([other, block], axis=axis),
            jnp.concatenate([block, other], axis=axis),
        )
    return block


def on_device(
    positions,
    leaf_centers,
    atom_counts,
    features,
    msg_weight,
    trans_weight,
    read_weight,
    pair_target,
    pair_source,
    pair_live,
    far_list,
):
    atom_num = positions.shape[1]
    all_bits = lax.axis_size("box").bit_length() - 1
    sub_bits = tuple(range(3))
    grp_bits = tuple(range(3, all_bits))
    index = lax.axis_index("box")
    groups = lax.axis_size("box") // 8
    group_id = index // 8
    slot_ids = jnp.arange(LEAF_ATOMS, dtype=jnp.int32)
    mask_f = (slot_ids[None, :] < atom_counts[:, None]).astype(jnp.float32).reshape(atom_num)
    hidden_t = (
        jnp.einsum("ic,ai->ca", msg_weight, features, preferred_element_type=jnp.float32)
        * mask_f[None, :]
    )
    pos_ext = extended(positions, (("box", 1),), atom_num)
    hid_ext = extended(hidden_t.astype(jnp.bfloat16), (("box", 1),), atom_num).astype(jnp.float32)

    def near_part(own, ext, feat_ext):
        return near_field(own, ext, feat_ext, pair_target, pair_source, pair_live)

    near_val, near_back = jax.vjp(near_part, positions, pos_ext, hid_ext)
    centers = jnp.repeat(leaf_centers, LEAF_ATOMS, axis=1)

    def far_basis(coords):
        return monomials((coords - centers) * REL_SCALE)

    basis_val, basis_back = jax.vjp(far_basis, positions)
    moment = jnp.einsum("ka,ca->kc", basis_val, hidden_t, precision=PRECISE)
    masked_feat = features.astype(jnp.float32) * mask_f[:, None]
    feat_basis = jnp.einsum("ka,ai->ki", basis_val, masked_feat, precision=PRECISE)
    counts_mat = jnp.sum(
        (far_list[:, :, None] == jnp.arange(groups, dtype=jnp.int32)[None, None, :]).astype(
            jnp.float32
        ),
        axis=1,
    )
    row_weights = lax.dynamic_index_in_dim(counts_mat, group_id, 0, keepdims=False)
    col_weights = lax.dynamic_index_in_dim(counts_mat, group_id, 1, keepdims=False)
    moment_part = split_sum(jnp.stack([moment, feat_basis]), index, sub_bits[::-1])
    moment_tab = tree_gather(moment_part[None], index, grp_bits, 0)
    mixed_part = jnp.einsum("j,jnkc->nkc", row_weights, moment_tab, precision=PRECISE)
    gathered_part = mixed_part[0]
    local_part = jnp.dot(trans_weight, gathered_part, precision=PRECISE)
    both = tree_gather(jnp.stack([local_part, mixed_part[1]]), index, sub_bits, 2)
    local_exp, feat_mixed = both[0], both[1]
    potential = jnp.einsum("ka,kc->ac", basis_val, local_exp, precision=PRECISE)
    pre_act = near_val + potential
    sigma = jax.nn.sigmoid(pre_act)
    activ = pre_act * sigma
    atom_energy = mask_f * jnp.dot(activ, read_weight, precision=PRECISE)
    d_pre = mask_f[:, None] * read_weight[None, :] * (sigma + pre_act * sigma * (1.0 - sigma))
    grad_read_part = jnp.dot(mask_f, activ, precision=PRECISE)
    d_local = jnp.dot(basis_val, d_pre, precision=PRECISE)
    d_basis = jnp.einsum("kc,ac->ka", local_exp, d_pre, precision=PRECISE)
    d_local_part = split_sum(d_local, index, sub_bits[::-1])
    grad_trans_part = jnp.einsum("kc,qc->kq", d_local_part, gathered_part, precision=PRECISE)
    d_gathered_part = jnp.dot(trans_weight.T, d_local_part, precision=PRECISE)
    slice_width = d_gathered_part.shape[1]
    far_msg_part = jnp.einsum("ki,kc->ic", feat_mixed, d_gathered_part, precision=PRECISE)
    far_msg = lax.dynamic_update_slice_in_dim(
        jnp.zeros((far_msg_part.shape[0], slice_width * 8), jnp.float32),
        far_msg_part,
        (index % 8) * slice_width,
        axis=1,
    )
    d_own, d_ext, d_feat_ext = near_back(d_pre)
    low_pos, low_feat = passed_along((d_ext[:, :atom_num], d_feat_ext[:, :atom_num]), "box", -1)
    high_pos, high_feat = (
        passed_along(d_ext[:, 2 * atom_num :].astype(jnp.bfloat16), "box", 1).astype(jnp.float32),
        passed_along(d_feat_ext[:, 2 * atom_num :].astype(jnp.bfloat16), "box", 1).astype(
            jnp.float32
        ),
    )
    d_hidden_near = d_feat_ext[:, atom_num : 2 * atom_num] + low_feat + high_feat
    grad_msg_part = (
        jnp.einsum("ai,ca->ic", masked_feat, d_hidden_near, precision=PRECISE) + far_msg
    )
    flat = jnp.concatenate(
        [grad_msg_part.reshape(-1), grad_trans_part.reshape(-1), grad_read_part.reshape(-1)]
    )
    d_tab, flat = tree_gather_sum(d_gathered_part[None], flat, index, grp_bits, 0)
    d_moment_part = jnp.einsum("b,bkc->kc", col_weights, d_tab, precision=PRECISE)
    d_moment, flat = tree_gather_sum(d_moment_part, flat, index, sub_bits, 1)
    d_basis = d_basis + jnp.dot(d_moment, hidden_t, precision=PRECISE)
    (d_far_pos,) = basis_back(d_basis)
    msg_size, trans_size = grad_msg_part.size, grad_trans_part.size
    grad_msg = flat[:msg_size].reshape(grad_msg_part.shape)
    grad_trans = flat[msg_size : msg_size + trans_size].reshape(grad_trans_part.shape)
    grad_read = flat[msg_size + trans_size :]
    forces = -(d_own + d_ext[:, atom_num : 2 * atom_num] + low_pos + high_pos + d_far_pos)
    return (atom_energy, forces, grad_msg, grad_trans, grad_read)


def solution(mesh):
    return jax.shard_map(
        on_device,
        mesh=mesh,
        in_specs=(
            P(None, "box"),
            P(None, "box"),
            P("box"),
            P("box", None),
            P(),
            P(),
            P(),
            P("box"),
            P("box"),
            P("box"),
            P(),
        ),
        out_specs=(P("box"), P(None, "box"), P(), P(), P()),
        check_vma=False,
    )
```

```python
import jax
import jax.numpy as jnp
from jax import lax
from jax.sharding import PartitionSpec as P

LEAF_ATOMS = 64
PAIR_LEAF = 27


PRECISE = lax.Precision.HIGHEST
GAMMA = 3.0
NEAR_SCALE = 0.3
REL_SCALE = 0.5
EXPONENTS = [
    (power_x, power_y, degree - power_x - power_y)
    for degree in range(5)
    for power_x in range(degree, -1, -1)
    for power_y in range(degree - power_x, -1, -1)
]


def extended(block, sides, width):
    for axis, dim in sides:
        count = lax.axis_size(axis)
        forward = [(i, i + 1) for i in range(count - 1)]
        backward = [(target, source) for source, target in forward]
        low = lax.ppermute(
            lax.slice_in_dim(block, block.shape[dim] - width, None, axis=dim), axis, forward
        )
        high = lax.ppermute(lax.slice_in_dim(block, 0, width, axis=dim), axis, backward)
        block = jnp.concatenate([low, block, high], axis=dim)
    return block


def passed_along(block, axis, distance):
    devices = range(lax.axis_size(axis))
    route = [(i - distance, i) for i in devices if i - distance in devices]
    return lax.ppermute(block, axis, route)


def monomials(relative):
    powers = []
    for axis_id in range(3):
        coords = relative[axis_id]
        stacked = [jnp.ones_like(coords), coords]
        for degree in range(2, 5):
            stacked.append(stacked[-1] * coords)
        powers.append(stacked)
    return jnp.stack(
        [powers[0][ex_a] * powers[1][ex_b] * powers[2][ex_c] for ex_a, ex_b, ex_c in EXPONENTS]
    )


def near_field(pos_own, pos_ext, hid_ext, targets, sources, alive):
    leaves = pos_own.shape[1] // LEAF_ATOMS
    channels = hid_ext.shape[0]
    own_leaf = pos_own.reshape(3, leaves, LEAF_ATOMS)
    ext_leaf = pos_ext.reshape(3, 3 * leaves, LEAF_ATOMS)
    feat_leaf = hid_ext.reshape(channels, 3 * leaves, LEAF_ATOMS)
    leaf_ids = jnp.arange(leaves, dtype=jnp.int32)
    blocks = (
        targets.reshape(-1, PAIR_LEAF),
        sources.reshape(-1, PAIR_LEAF),
        alive.reshape(-1, PAIR_LEAF),
    )

    def one_block(accumulated, pair_block):
        tgt_ids, src_ids, live_ids = pair_block
        near_pos = own_leaf[:, tgt_ids]
        far_pos = ext_leaf[:, src_ids]
        dist_sq = jnp.zeros((tgt_ids.shape[0], LEAF_ATOMS, LEAF_ATOMS), jnp.float32)
        for axis_id in range(3):
            offset_ax = near_pos[axis_id][:, :, None] - far_pos[axis_id][:, None, :]
            dist_sq = dist_sq + offset_ax * offset_ax
        kernel = (
            NEAR_SCALE * jnp.exp(-GAMMA * dist_sq) * live_ids.astype(jnp.float32)[:, None, None]
        ).astype(jnp.bfloat16)
        source_feat = feat_leaf[:, src_ids].astype(jnp.bfloat16)
        contrib = jnp.einsum(
            "pij,cpj->pic", kernel, source_feat, preferred_element_type=jnp.float32
        )
        onehot = (tgt_ids[None, :] == leaf_ids[:, None]).astype(jnp.float32)
        return (accumulated + jnp.einsum("tp,pic->tic", onehot, contrib, precision=PRECISE), None)

    initial = jnp.zeros((leaves, LEAF_ATOMS, channels), jnp.float32)
    accumulated, unused = lax.scan(jax.checkpoint(one_block), initial, blocks)
    return accumulated.reshape(leaves * LEAF_ATOMS, channels)


def xor_swap(block, bit):
    count = lax.axis_size("box")
    return lax.ppermute(block, "box", [(i, i ^ (1 << bit)) for i in range(count)])


def tree_sum(block, bits):
    for bit in bits:
        block = block + xor_swap(block, bit)
    return block


def split_sum(block, index, bits):
    for bit in bits:
        half = block.shape[-1] // 2
        lower, upper = block[..., :half], block[..., half:]
        up = ((index >> bit) & 1) == 1
        keep = jnp.where(up, upper, lower)
        send = jnp.where(up, lower, upper)
        block = keep + xor_swap(send, bit)
    return block


def tree_gather_sum(block, extra, index, bits, axis):
    for bit in bits:
        packed = xor_swap(jnp.concatenate([block.reshape(-1), extra]), bit)
        other = packed[: block.size].reshape(block.shape)
        other_extra = packed[block.size :]
        up = ((index >> bit) & 1) == 1
        block = jnp.where(
            up,
            jnp.concatenate([other, block], axis=axis),
            jnp.concatenate([block, other], axis=axis),
        )
        extra = extra + other_extra
    return block, extra


def tree_gather(block, index, bits, axis):
    for bit in bits:
        other = xor_swap(block, bit)
        up = ((index >> bit) & 1) == 1
        block = jnp.where(
            up,
            jnp.concatenate([other, block], axis=axis),
            jnp.concatenate([block, other], axis=axis),
        )
    return block


def on_device(
    positions,
    leaf_centers,
    atom_counts,
    features,
    msg_weight,
    trans_weight,
    read_weight,
    pair_target,
    pair_source,
    pair_live,
    far_list,
):
    atom_num = positions.shape[1]
    all_bits = lax.axis_size("box").bit_length() - 1
    sub_bits = tuple(range(3))
    grp_bits = tuple(range(3, all_bits))
    index = lax.axis_index("box")
    groups = lax.axis_size("box") // 8
    group_id = index // 8
    slot_ids = jnp.arange(LEAF_ATOMS, dtype=jnp.int32)
    mask_f = (slot_ids[None, :] < atom_counts[:, None]).astype(jnp.float32).reshape(atom_num)
    hidden_t = (
        jnp.einsum("ic,ai->ca", msg_weight, features, preferred_element_type=jnp.float32)
        * mask_f[None, :]
    )
    pos_ext = extended(positions, (("box", 1),), atom_num)
    hid_ext = extended(hidden_t.astype(jnp.bfloat16), (("box", 1),), atom_num).astype(jnp.float32)

    def near_part(own, ext, feat_ext):
        return near_field(own, ext, feat_ext, pair_target, pair_source, pair_live)

    near_val, near_back = jax.vjp(near_part, positions, pos_ext, hid_ext)
    centers = jnp.repeat(leaf_centers, LEAF_ATOMS, axis=1)

    def far_basis(coords):
        return monomials((coords - centers) * REL_SCALE)

    basis_val, basis_back = jax.vjp(far_basis, positions)
    moment = jnp.einsum("ka,ca->kc", basis_val, hidden_t, precision=PRECISE)
    masked_feat = features.astype(jnp.float32) * mask_f[:, None]
    feat_basis = jnp.einsum("ka,ai->ki", basis_val, masked_feat, precision=PRECISE)
    counts_mat = jnp.sum(
        (far_list[:, :, None] == jnp.arange(groups, dtype=jnp.int32)[None, None, :]).astype(
            jnp.float32
        ),
        axis=1,
    )
    row_weights = lax.dynamic_index_in_dim(counts_mat, group_id, 0, keepdims=False)
    col_weights = lax.dynamic_index_in_dim(counts_mat, group_id, 1, keepdims=False)
    moment_part = split_sum(jnp.stack([moment, feat_basis]), index, sub_bits[::-1])
    moment_tab = tree_gather(moment_part[None], index, grp_bits, 0)
    mixed_part = jnp.einsum("j,jnkc->nkc", row_weights, moment_tab, precision=PRECISE)
    gathered_part = mixed_part[0]
    local_part = jnp.dot(trans_weight, gathered_part, precision=PRECISE)
    both = tree_gather(jnp.stack([local_part, mixed_part[1]]), index, sub_bits, 2)
    local_exp, feat_mixed = both[0], both[1]
    potential = jnp.einsum("ka,kc->ac", basis_val, local_exp, precision=PRECISE)
    pre_act = near_val + potential
    sigma = jax.nn.sigmoid(pre_act)
    activ = pre_act * sigma
    atom_energy = mask_f * jnp.dot(activ, read_weight, precision=PRECISE)
    d_pre = mask_f[:, None] * read_weight[None, :] * (sigma + pre_act * sigma * (1.0 - sigma))
    grad_read_part = jnp.dot(mask_f, activ, precision=PRECISE)
    d_local = jnp.dot(basis_val, d_pre, precision=PRECISE)
    d_basis = jnp.einsum("kc,ac->ka", local_exp, d_pre, precision=PRECISE)
    d_local_part = split_sum(d_local, index, sub_bits[::-1])
    grad_trans_part = jnp.einsum("kc,qc->kq", d_local_part, gathered_part, precision=PRECISE)
    d_gathered_part = jnp.dot(trans_weight.T, d_local_part, precision=PRECISE)
    slice_width = d_gathered_part.shape[1]
    far_msg_part = jnp.einsum("ki,kc->ic", feat_mixed, d_gathered_part, precision=PRECISE)
    far_msg = lax.dynamic_update_slice_in_dim(
        jnp.zeros((far_msg_part.shape[0], slice_width * 8), jnp.float32),
        far_msg_part,
        (index % 8) * slice_width,
        axis=1,
    )
    d_own, d_ext, d_feat_ext = near_back(d_pre)
    low_pos, low_feat = passed_along((d_ext[:, :atom_num], d_feat_ext[:, :atom_num]), "box", -1)
    high_pos, high_feat = (
        passed_along(d_ext[:, 2 * atom_num :].astype(jnp.bfloat16), "box", 1).astype(jnp.float32),
        passed_along(d_feat_ext[:, 2 * atom_num :].astype(jnp.bfloat16), "box", 1).astype(
            jnp.float32
        ),
    )
    d_hidden_near = d_feat_ext[:, atom_num : 2 * atom_num] + low_feat + high_feat
    grad_msg_part = (
        jnp.einsum("ai,ca->ic", masked_feat, d_hidden_near, precision=PRECISE) + far_msg
    )
    flat = jnp.concatenate(
        [grad_msg_part.reshape(-1), grad_trans_part.reshape(-1), grad_read_part.reshape(-1)]
    )
    d_tab, flat = tree_gather_sum(d_gathered_part[None], flat, index, grp_bits, 0)
    d_moment_part = jnp.einsum("b,bkc->kc", col_weights, d_tab, precision=PRECISE)
    d_moment, flat = tree_gather_sum(d_moment_part, flat, index, sub_bits, 1)
    d_basis = d_basis + jnp.dot(d_moment, hidden_t, precision=PRECISE)
    (d_far_pos,) = basis_back(d_basis)
    msg_size, trans_size = grad_msg_part.size, grad_trans_part.size
    grad_msg = flat[:msg_size].reshape(grad_msg_part.shape)
    grad_trans = flat[msg_size : msg_size + trans_size].reshape(grad_trans_part.shape)
    grad_read = flat[msg_size + trans_size :]
    forces = -(d_own + d_ext[:, atom_num : 2 * atom_num] + low_pos + high_pos + d_far_pos)
    return (atom_energy, forces, grad_msg, grad_trans, grad_read)


def solution(mesh):
    return jax.shard_map(
        on_device,
        mesh=mesh,
        in_specs=(
            P(None, "box"),
            P(None, "box"),
            P("box"),
            P("box", None),
            P(),
            P(),
            P(),
            P("box"),
            P("box"),
            P("box"),
            P(),
        ),
        out_specs=(P("box"), P(None, "box"), P(), P(), P()),
        check_vma=False,
    )
```

```python
import jax
import jax.numpy as jnp
from jax import lax
from jax.sharding import PartitionSpec as P

LEAF_ATOMS = 64
PAIR_LEAF = 27


PRECISE = lax.Precision.HIGHEST
GAMMA = 3.0
NEAR_SCALE = 0.3
REL_SCALE = 0.5
EXPONENTS = [
    (power_x, power_y, degree - power_x - power_y)
    for degree in range(5)
    for power_x in range(degree, -1, -1)
    for power_y in range(degree - power_x, -1, -1)
]


def extended(block, sides, width):
    for axis, dim in sides:
        count = lax.axis_size(axis)
        forward = [(i, i + 1) for i in range(count - 1)]
        backward = [(target, source) for source, target in forward]
        low = lax.ppermute(
            lax.slice_in_dim(block, block.shape[dim] - width, None, axis=dim), axis, forward
        )
        high = lax.ppermute(lax.slice_in_dim(block, 0, width, axis=dim), axis, backward)
        block = jnp.concatenate([low, block, high], axis=dim)
    return block


def passed_along(block, axis, distance):
    devices = range(lax.axis_size(axis))
    route = [(i - distance, i) for i in devices if i - distance in devices]
    return lax.ppermute(block, axis, route)


def monomials(relative):
    powers = []
    for axis_id in range(3):
        coords = relative[axis_id]
        stacked = [jnp.ones_like(coords), coords]
        for degree in range(2, 5):
            stacked.append(stacked[-1] * coords)
        powers.append(stacked)
    return jnp.stack(
        [powers[0][ex_a] * powers[1][ex_b] * powers[2][ex_c] for ex_a, ex_b, ex_c in EXPONENTS]
    )


def near_field(pos_own, pos_ext, hid_ext, targets, sources, alive):
    leaves = pos_own.shape[1] // LEAF_ATOMS
    channels = hid_ext.shape[0]
    own_leaf = pos_own.reshape(3, leaves, LEAF_ATOMS)
    ext_leaf = pos_ext.reshape(3, 3 * leaves, LEAF_ATOMS)
    feat_leaf = hid_ext.reshape(channels, 3 * leaves, LEAF_ATOMS)
    tgt_hot = (targets[:, None] == jnp.arange(leaves, dtype=jnp.int32)[None, :]).astype(
        jnp.float32
    )
    src_hot = (sources[:, None] == jnp.arange(3 * leaves, dtype=jnp.int32)[None, :]).astype(
        jnp.float32
    )
    near_pos = jnp.einsum("pt,xti->xpi", tgt_hot, own_leaf, precision=PRECISE)
    far_pos = jnp.einsum("ps,xsj->xpj", src_hot, ext_leaf, precision=PRECISE)
    dist_sq = jnp.zeros((targets.shape[0], LEAF_ATOMS, LEAF_ATOMS), jnp.float32)
    for axis_id in range(3):
        offset_ax = near_pos[axis_id][:, :, None] - far_pos[axis_id][:, None, :]
        dist_sq = dist_sq + offset_ax * offset_ax
    kernel = (
        NEAR_SCALE * jnp.exp(-GAMMA * dist_sq) * alive.astype(jnp.float32)[:, None, None]
    ).astype(jnp.bfloat16)
    source_feat = jnp.einsum("ps,csj->pjc", src_hot, feat_leaf, precision=PRECISE).astype(
        jnp.bfloat16
    )
    contrib = jnp.einsum("pij,pjc->pic", kernel, source_feat, preferred_element_type=jnp.float32)
    accumulated = jnp.einsum("pt,pic->tic", tgt_hot, contrib, precision=PRECISE)
    return accumulated.reshape(leaves * LEAF_ATOMS, channels)


def xor_swap(block, bit):
    count = lax.axis_size("box")
    return lax.ppermute(block, "box", [(i, i ^ (1 << bit)) for i in range(count)])


def tree_sum(block, bits):
    for bit in bits:
        block = block + xor_swap(block, bit)
    return block


def split_sum(block, index, bits):
    for bit in bits:
        half = block.shape[-1] // 2
        lower, upper = block[..., :half], block[..., half:]
        up = ((index >> bit) & 1) == 1
        keep = jnp.where(up, upper, lower)
        send = jnp.where(up, lower, upper)
        block = keep + xor_swap(send, bit)
    return block


def tree_gather_sum(block, extra, index, bits, axis):
    for bit in bits:
        packed = xor_swap(jnp.concatenate([block.reshape(-1), extra]), bit)
        other = packed[: block.size].reshape(block.shape)
        other_extra = packed[block.size :]
        up = ((index >> bit) & 1) == 1
        block = jnp.where(
            up,
            jnp.concatenate([other, block], axis=axis),
            jnp.concatenate([block, other], axis=axis),
        )
        extra = extra + other_extra
    return block, extra


def tree_gather(block, index, bits, axis):
    for bit in bits:
        other = xor_swap(block, bit)
        up = ((index >> bit) & 1) == 1
        block = jnp.where(
            up,
            jnp.concatenate([other, block], axis=axis),
            jnp.concatenate([block, other], axis=axis),
        )
    return block


def on_device(
    positions,
    leaf_centers,
    atom_counts,
    features,
    msg_weight,
    trans_weight,
    read_weight,
    pair_target,
    pair_source,
    pair_live,
    far_list,
):
    atom_num = positions.shape[1]
    all_bits = lax.axis_size("box").bit_length() - 1
    sub_bits = tuple(range(3))
    grp_bits = tuple(range(3, all_bits))
    index = lax.axis_index("box")
    groups = lax.axis_size("box") // 8
    group_id = index // 8
    slot_ids = jnp.arange(LEAF_ATOMS, dtype=jnp.int32)
    mask_f = (slot_ids[None, :] < atom_counts[:, None]).astype(jnp.float32).reshape(atom_num)
    hidden_t = (
        jnp.einsum("ic,ai->ca", msg_weight, features, preferred_element_type=jnp.float32)
        * mask_f[None, :]
    )
    pos_ext = extended(positions, (("box", 1),), atom_num)
    hid_ext = extended(hidden_t.astype(jnp.bfloat16), (("box", 1),), atom_num).astype(jnp.float32)

    def near_part(own, ext, feat_ext):
        return near_field(own, ext, feat_ext, pair_target, pair_source, pair_live)

    near_val, near_back = jax.vjp(near_part, positions, pos_ext, hid_ext)
    centers = jnp.repeat(leaf_centers, LEAF_ATOMS, axis=1)

    def far_basis(coords):
        return monomials((coords - centers) * REL_SCALE)

    basis_val, basis_back = jax.vjp(far_basis, positions)
    moment = jnp.einsum("ka,ca->kc", basis_val, hidden_t, precision=PRECISE)
    masked_feat = features.astype(jnp.float32) * mask_f[:, None]
    feat_basis = jnp.einsum("ka,ai->ki", basis_val, masked_feat, precision=PRECISE)
    counts_mat = jnp.sum(
        (far_list[:, :, None] == jnp.arange(groups, dtype=jnp.int32)[None, None, :]).astype(
            jnp.float32
        ),
        axis=1,
    )
    row_weights = lax.dynamic_index_in_dim(counts_mat, group_id, 0, keepdims=False)
    col_weights = lax.dynamic_index_in_dim(counts_mat, group_id, 1, keepdims=False)
    moment_part = split_sum(jnp.stack([moment, feat_basis]), index, sub_bits[::-1])
    moment_tab = tree_gather(moment_part[None], index, grp_bits, 0)
    mixed_part = jnp.einsum("j,jnkc->nkc", row_weights, moment_tab, precision=PRECISE)
    gathered_part = mixed_part[0]
    local_part = jnp.dot(trans_weight, gathered_part, precision=PRECISE)
    both = tree_gather(jnp.stack([local_part, mixed_part[1]]), index, sub_bits, 2)
    local_exp, feat_mixed = both[0], both[1]
    potential = jnp.einsum("ka,kc->ac", basis_val, local_exp, precision=PRECISE)
    pre_act = near_val + potential
    sigma = jax.nn.sigmoid(pre_act)
    activ = pre_act * sigma
    atom_energy = mask_f * jnp.dot(activ, read_weight, precision=PRECISE)
    d_pre = mask_f[:, None] * read_weight[None, :] * (sigma + pre_act * sigma * (1.0 - sigma))
    grad_read_part = jnp.dot(mask_f, activ, precision=PRECISE)
    d_local = jnp.dot(basis_val, d_pre, precision=PRECISE)
    d_basis = jnp.einsum("kc,ac->ka", local_exp, d_pre, precision=PRECISE)
    d_local_part = split_sum(d_local, index, sub_bits[::-1])
    grad_trans_part = jnp.einsum("kc,qc->kq", d_local_part, gathered_part, precision=PRECISE)
    d_gathered_part = jnp.dot(trans_weight.T, d_local_part, precision=PRECISE)
    slice_width = d_gathered_part.shape[1]
    far_msg_part = jnp.einsum("ki,kc->ic", feat_mixed, d_gathered_part, precision=PRECISE)
    far_msg = lax.dynamic_update_slice_in_dim(
        jnp.zeros((far_msg_part.shape[0], slice_width * 8), jnp.float32),
        far_msg_part,
        (index % 8) * slice_width,
        axis=1,
    )
    d_own, d_ext, d_feat_ext = near_back(d_pre)
    low_pos, low_feat = passed_along((d_ext[:, :atom_num], d_feat_ext[:, :atom_num]), "box", -1)
    high_pos, high_feat = (
        passed_along(d_ext[:, 2 * atom_num :].astype(jnp.bfloat16), "box", 1).astype(jnp.float32),
        passed_along(d_feat_ext[:, 2 * atom_num :].astype(jnp.bfloat16), "box", 1).astype(
            jnp.float32
        ),
    )
    d_hidden_near = d_feat_ext[:, atom_num : 2 * atom_num] + low_feat + high_feat
    grad_msg_part = (
        jnp.einsum("ai,ca->ic", masked_feat, d_hidden_near, precision=PRECISE) + far_msg
    )
    flat = jnp.concatenate(
        [grad_msg_part.reshape(-1), grad_trans_part.reshape(-1), grad_read_part.reshape(-1)]
    )
    d_tab, flat = tree_gather_sum(d_gathered_part[None], flat, index, grp_bits, 0)
    d_moment_part = jnp.einsum("b,bkc->kc", col_weights, d_tab, precision=PRECISE)
    d_moment, flat = tree_gather_sum(d_moment_part, flat, index, sub_bits, 1)
    d_basis = d_basis + jnp.dot(d_moment, hidden_t, precision=PRECISE)
    (d_far_pos,) = basis_back(d_basis)
    msg_size, trans_size = grad_msg_part.size, grad_trans_part.size
    grad_msg = flat[:msg_size].reshape(grad_msg_part.shape)
    grad_trans = flat[msg_size : msg_size + trans_size].reshape(grad_trans_part.shape)
    grad_read = flat[msg_size + trans_size :]
    forces = -(d_own + d_ext[:, atom_num : 2 * atom_num] + low_pos + high_pos + d_far_pos)
    return (atom_energy, forces, grad_msg, grad_trans, grad_read)


def solution(mesh):
    return jax.shard_map(
        on_device,
        mesh=mesh,
        in_specs=(
            P(None, "box"),
            P(None, "box"),
            P("box"),
            P("box", None),
            P(),
            P(),
            P(),
            P("box"),
            P("box"),
            P("box"),
            P(),
        ),
        out_specs=(P("box"), P(None, "box"), P(), P(), P()),
        check_vma=False,
    )
```

```python
import jax
import jax.numpy as jnp
from jax import lax
from jax.sharding import PartitionSpec as P

LEAF_ATOMS = 64
PAIR_LEAF = 27


PRECISE = lax.Precision.HIGHEST
GAMMA = 3.0
NEAR_SCALE = 0.3
REL_SCALE = 0.5
EXPONENTS = [
    (power_x, power_y, degree - power_x - power_y)
    for degree in range(5)
    for power_x in range(degree, -1, -1)
    for power_y in range(degree - power_x, -1, -1)
]


def extended(block, sides, width):
    for axis, dim in sides:
        count = lax.axis_size(axis)
        forward = [(i, i + 1) for i in range(count - 1)]
        backward = [(target, source) for source, target in forward]
        low = lax.ppermute(
            lax.slice_in_dim(block, block.shape[dim] - width, None, axis=dim), axis, forward
        )
        high = lax.ppermute(lax.slice_in_dim(block, 0, width, axis=dim), axis, backward)
        block = jnp.concatenate([low, block, high], axis=dim)
    return block


def passed_along(block, axis, distance):
    devices = range(lax.axis_size(axis))
    route = [(i - distance, i) for i in devices if i - distance in devices]
    return lax.ppermute(block, axis, route)


def monomials(relative):
    powers = []
    for axis_id in range(3):
        coords = relative[axis_id]
        stacked = [jnp.ones_like(coords), coords]
        for degree in range(2, 5):
            stacked.append(stacked[-1] * coords)
        powers.append(stacked)
    return jnp.stack(
        [powers[0][ex_a] * powers[1][ex_b] * powers[2][ex_c] for ex_a, ex_b, ex_c in EXPONENTS]
    )


def near_field(pos_own, pos_ext, hid_ext, targets, sources, alive):
    leaves = pos_own.shape[1] // LEAF_ATOMS
    channels = hid_ext.shape[0]
    own_leaf = pos_own.reshape(3, leaves, LEAF_ATOMS)
    ext_leaf = pos_ext.reshape(3, 3 * leaves, LEAF_ATOMS)
    feat_leaf = hid_ext.reshape(channels, 3 * leaves, LEAF_ATOMS)
    tgt_hot = (targets[:, None] == jnp.arange(leaves, dtype=jnp.int32)[None, :]).astype(
        jnp.float32
    )
    src_hot = (sources[:, None] == jnp.arange(3 * leaves, dtype=jnp.int32)[None, :]).astype(
        jnp.float32
    )
    near_pos = jnp.einsum("pt,xti->xpi", tgt_hot, own_leaf, precision=PRECISE)
    far_pos = jnp.einsum("ps,xsj->xpj", src_hot, ext_leaf, precision=PRECISE)
    dist_sq = jnp.zeros((targets.shape[0], LEAF_ATOMS, LEAF_ATOMS), jnp.float32)
    for axis_id in range(3):
        offset_ax = near_pos[axis_id][:, :, None] - far_pos[axis_id][:, None, :]
        dist_sq = dist_sq + offset_ax * offset_ax
    kernel = (
        NEAR_SCALE * jnp.exp(-GAMMA * dist_sq) * alive.astype(jnp.float32)[:, None, None]
    ).astype(jnp.bfloat16)
    source_feat = jnp.einsum("ps,csj->pjc", src_hot, feat_leaf, precision=PRECISE).astype(
        jnp.bfloat16
    )
    contrib = jnp.einsum("pij,pjc->pic", kernel, source_feat, preferred_element_type=jnp.float32)
    accumulated = jnp.einsum("pt,pic->tic", tgt_hot, contrib, precision=PRECISE)
    return accumulated.reshape(leaves * LEAF_ATOMS, channels)


def member_of(index, bits):
    return sum(((index >> bit) & 1) << place for place, bit in enumerate(bits))


def bits_mask(member, bits):
    return sum(((member >> place) & 1) << bit for place, bit in enumerate(bits))


def swap_with(block, mask):
    count = lax.axis_size("box")
    return lax.ppermute(block, "box", [(i, i ^ mask) for i in range(count)])


def round_split(block, index, bits):
    me = member_of(index, bits)
    size = 1 << len(bits)
    width = block.shape[-1] // size
    slices = jnp.stack([block[..., q * width : (q + 1) * width] for q in range(size)])
    total = slices[me]
    for member in range(1, size):
        total = total + swap_with(slices[me ^ member], bits_mask(member, bits))
    return total


def round_gather(block, extra, index, bits, axis):
    me = member_of(index, bits)
    size = 1 << len(bits)
    own = block.reshape(-1) if extra is None else jnp.concatenate([block.reshape(-1), extra])
    received = [own] + [swap_with(own, bits_mask(member, bits)) for member in range(1, size)]
    ordered = jnp.take(jnp.stack(received), jnp.arange(size, dtype=jnp.int32) ^ me, axis=0)
    gathered = jnp.concatenate(
        [ordered[q, : block.size].reshape(block.shape) for q in range(size)], axis=axis
    )
    if extra is None:
        return gathered
    total = ordered[0, block.size :]
    for q in range(1, size):
        total = total + ordered[q, block.size :]
    return gathered, total


def on_device(
    positions,
    leaf_centers,
    atom_counts,
    features,
    msg_weight,
    trans_weight,
    read_weight,
    pair_target,
    pair_source,
    pair_live,
    far_list,
):
    atom_num = positions.shape[1]
    all_bits = lax.axis_size("box").bit_length() - 1
    sub_bits = (0, 1, 2)
    grp_rounds = [tuple(range(low, min(low + 3, all_bits))) for low in range(3, all_bits, 3)]
    index = lax.axis_index("box")
    groups = lax.axis_size("box") // 8
    group_id = index // 8
    slot_ids = jnp.arange(LEAF_ATOMS, dtype=jnp.int32)
    mask_f = (slot_ids[None, :] < atom_counts[:, None]).astype(jnp.float32).reshape(atom_num)
    hidden_t = (
        jnp.einsum("ic,ai->ca", msg_weight, features, preferred_element_type=jnp.float32)
        * mask_f[None, :]
    )
    pos_ext = extended(positions, (("box", 1),), atom_num)
    hid_ext = extended(hidden_t.astype(jnp.bfloat16), (("box", 1),), atom_num).astype(jnp.float32)

    def near_part(own, ext, feat_ext):
        return near_field(own, ext, feat_ext, pair_target, pair_source, pair_live)

    near_val, near_back = jax.vjp(near_part, positions, pos_ext, hid_ext)
    centers = jnp.repeat(leaf_centers, LEAF_ATOMS, axis=1)

    def far_basis(coords):
        return monomials((coords - centers) * REL_SCALE)

    basis_val, basis_back = jax.vjp(far_basis, positions)
    moment = jnp.einsum("ka,ca->kc", basis_val, hidden_t, precision=PRECISE)
    masked_feat = features.astype(jnp.float32) * mask_f[:, None]
    feat_basis = jnp.einsum("ka,ai->ki", basis_val, masked_feat, precision=PRECISE)
    counts_mat = jnp.sum(
        (far_list[:, :, None] == jnp.arange(groups, dtype=jnp.int32)[None, None, :]).astype(
            jnp.float32
        ),
        axis=1,
    )
    row_weights = lax.dynamic_index_in_dim(counts_mat, group_id, 0, keepdims=False)
    col_weights = lax.dynamic_index_in_dim(counts_mat, group_id, 1, keepdims=False)
    moment_tab = round_split(jnp.stack([moment, feat_basis]), index, sub_bits)[None]
    for bits in grp_rounds:
        moment_tab = round_gather(moment_tab, None, index, bits, 0)
    mixed_part = jnp.einsum("j,jnkc->nkc", row_weights, moment_tab, precision=PRECISE)
    gathered_part = mixed_part[0]
    local_part = jnp.dot(trans_weight, gathered_part, precision=PRECISE)
    both = round_gather(jnp.stack([local_part, mixed_part[1]]), None, index, sub_bits, 2)
    local_exp, feat_mixed = both[0], both[1]
    potential = jnp.einsum("ka,kc->ac", basis_val, local_exp, precision=PRECISE)
    pre_act = near_val + potential
    sigma = jax.nn.sigmoid(pre_act)
    activ = pre_act * sigma
    atom_energy = mask_f * jnp.dot(activ, read_weight, precision=PRECISE)
    d_pre = mask_f[:, None] * read_weight[None, :] * (sigma + pre_act * sigma * (1.0 - sigma))
    grad_read_part = jnp.dot(mask_f, activ, precision=PRECISE)
    d_local = jnp.dot(basis_val, d_pre, precision=PRECISE)
    d_basis = jnp.einsum("kc,ac->ka", local_exp, d_pre, precision=PRECISE)
    d_local_part = round_split(d_local, index, sub_bits)
    grad_trans_part = jnp.einsum("kc,qc->kq", d_local_part, gathered_part, precision=PRECISE)
    d_gathered_part = jnp.dot(trans_weight.T, d_local_part, precision=PRECISE)
    slice_width = d_gathered_part.shape[1]
    far_msg_part = jnp.einsum("ki,kc->ic", feat_mixed, d_gathered_part, precision=PRECISE)
    far_msg = lax.dynamic_update_slice_in_dim(
        jnp.zeros((far_msg_part.shape[0], slice_width * 8), jnp.float32),
        far_msg_part,
        (index % 8) * slice_width,
        axis=1,
    )
    d_own, d_ext, d_feat_ext = near_back(d_pre)
    low_pos, low_feat = passed_along((d_ext[:, :atom_num], d_feat_ext[:, :atom_num]), "box", -1)
    high_pos, high_feat = (
        passed_along(d_ext[:, 2 * atom_num :].astype(jnp.bfloat16), "box", 1).astype(jnp.float32),
        passed_along(d_feat_ext[:, 2 * atom_num :].astype(jnp.bfloat16), "box", 1).astype(
            jnp.float32
        ),
    )
    d_hidden_near = d_feat_ext[:, atom_num : 2 * atom_num] + low_feat + high_feat
    grad_msg_part = (
        jnp.einsum("ai,ca->ic", masked_feat, d_hidden_near, precision=PRECISE) + far_msg
    )
    flat = jnp.concatenate(
        [grad_msg_part.reshape(-1), grad_trans_part.reshape(-1), grad_read_part.reshape(-1)]
    )
    d_tab = d_gathered_part[None]
    for bits in grp_rounds:
        d_tab, flat = round_gather(d_tab, flat, index, bits, 0)
    d_moment_part = jnp.einsum("b,bkc->kc", col_weights, d_tab, precision=PRECISE)
    d_moment, flat = round_gather(d_moment_part, flat, index, sub_bits, 1)
    d_basis = d_basis + jnp.dot(d_moment, hidden_t, precision=PRECISE)
    (d_far_pos,) = basis_back(d_basis)
    msg_size, trans_size = grad_msg_part.size, grad_trans_part.size
    grad_msg = flat[:msg_size].reshape(grad_msg_part.shape)
    grad_trans = flat[msg_size : msg_size + trans_size].reshape(grad_trans_part.shape)
    grad_read = flat[msg_size + trans_size :]
    forces = -(d_own + d_ext[:, atom_num : 2 * atom_num] + low_pos + high_pos + d_far_pos)
    return (atom_energy, forces, grad_msg, grad_trans, grad_read)


def solution(mesh):
    return jax.shard_map(
        on_device,
        mesh=mesh,
        in_specs=(
            P(None, "box"),
            P(None, "box"),
            P("box"),
            P("box", None),
            P(),
            P(),
            P(),
            P("box"),
            P("box"),
            P("box"),
            P(),
        ),
        out_specs=(P("box"), P(None, "box"), P(), P(), P()),
        check_vma=False,
    )
```

```python
import jax
import jax.numpy as jnp
from jax import lax
from jax.sharding import PartitionSpec as P

LEAF_ATOMS = 64
PAIR_LEAF = 27


PRECISE = lax.Precision.HIGHEST
GAMMA = 3.0
NEAR_SCALE = 0.3
REL_SCALE = 0.5
EXPONENTS = [
    (power_x, power_y, degree - power_x - power_y)
    for degree in range(5)
    for power_x in range(degree, -1, -1)
    for power_y in range(degree - power_x, -1, -1)
]


def extended(block, sides, width):
    for axis, dim in sides:
        count = lax.axis_size(axis)
        forward = [(i, i + 1) for i in range(count - 1)]
        backward = [(target, source) for source, target in forward]
        low = lax.ppermute(
            lax.slice_in_dim(block, block.shape[dim] - width, None, axis=dim), axis, forward
        )
        high = lax.ppermute(lax.slice_in_dim(block, 0, width, axis=dim), axis, backward)
        block = jnp.concatenate([low, block, high], axis=dim)
    return block


def passed_along(block, axis, distance):
    devices = range(lax.axis_size(axis))
    route = [(i - distance, i) for i in devices if i - distance in devices]
    return lax.ppermute(block, axis, route)


def monomials(relative):
    powers = []
    for axis_id in range(3):
        coords = relative[axis_id]
        stacked = [jnp.ones_like(coords), coords]
        for degree in range(2, 5):
            stacked.append(stacked[-1] * coords)
        powers.append(stacked)
    return jnp.stack(
        [powers[0][ex_a] * powers[1][ex_b] * powers[2][ex_c] for ex_a, ex_b, ex_c in EXPONENTS]
    )


def near_field(pos_own, pos_ext, hid_ext, targets, sources, alive):
    leaves = pos_own.shape[1] // LEAF_ATOMS
    channels = hid_ext.shape[0]
    own_leaf = pos_own.reshape(3, leaves, LEAF_ATOMS)
    ext_leaf = pos_ext.reshape(3, 3 * leaves, LEAF_ATOMS)
    feat_leaf = hid_ext.reshape(channels, 3 * leaves, LEAF_ATOMS)
    tgt_hot = (targets[:, None] == jnp.arange(leaves, dtype=jnp.int32)[None, :]).astype(
        jnp.float32
    )
    src_hot = (sources[:, None] == jnp.arange(3 * leaves, dtype=jnp.int32)[None, :]).astype(
        jnp.float32
    )
    near_pos = jnp.einsum("pt,xti->xpi", tgt_hot, own_leaf, precision=PRECISE)
    far_pos = jnp.einsum("ps,xsj->xpj", src_hot, ext_leaf, precision=PRECISE)
    dist_sq = jnp.zeros((targets.shape[0], LEAF_ATOMS, LEAF_ATOMS), jnp.float32)
    for axis_id in range(3):
        offset_ax = near_pos[axis_id][:, :, None] - far_pos[axis_id][:, None, :]
        dist_sq = dist_sq + offset_ax * offset_ax
    kernel = (
        NEAR_SCALE * jnp.exp(-GAMMA * dist_sq) * alive.astype(jnp.float32)[:, None, None]
    ).astype(jnp.bfloat16)
    source_feat = jnp.einsum("ps,csj->pjc", src_hot, feat_leaf, precision=PRECISE).astype(
        jnp.bfloat16
    )
    contrib = jnp.einsum("pij,pjc->pic", kernel, source_feat, preferred_element_type=jnp.float32)
    accumulated = jnp.einsum("pt,pic->tic", tgt_hot, contrib, precision=PRECISE)
    return accumulated.reshape(leaves * LEAF_ATOMS, channels)


def xor_swap(block, bit):
    count = lax.axis_size("box")
    return lax.ppermute(block, "box", [(i, i ^ (1 << bit)) for i in range(count)])


def split_sum(block, index, bits):
    for bit in bits:
        half = block.shape[0] // 2
        lower, upper = block[:half], block[half:]
        up = ((index >> bit) & 1) == 1
        keep = jnp.where(up, upper, lower)
        send = jnp.where(up, lower, upper)
        block = keep + xor_swap(send, bit)
    return block


def tree_gather_sum(block, extra, index, bits):
    for bit in bits:
        packed = xor_swap(jnp.concatenate([block, extra]), bit)
        other, other_extra = packed[: block.size], packed[block.size :]
        up = ((index >> bit) & 1) == 1
        block = jnp.where(
            up, jnp.concatenate([other, block]), jnp.concatenate([block, other])
        )
        extra = extra + other_extra
    return block, extra


def tree_gather(block, index, bits):
    for bit in bits:
        other = xor_swap(block, bit)
        up = ((index >> bit) & 1) == 1
        block = jnp.where(
            up, jnp.concatenate([other, block]), jnp.concatenate([block, other])
        )
    return block


def on_device(
    positions,
    leaf_centers,
    atom_counts,
    features,
    msg_weight,
    trans_weight,
    read_weight,
    pair_target,
    pair_source,
    pair_live,
    far_list,
):
    atom_num = positions.shape[1]
    all_bits = lax.axis_size("box").bit_length() - 1
    sub_bits = tuple(range(3))
    grp_bits = tuple(range(3, all_bits))
    index = lax.axis_index("box")
    groups = lax.axis_size("box") // 8
    group_id = index // 8
    slot_ids = jnp.arange(LEAF_ATOMS, dtype=jnp.int32)
    mask_f = (slot_ids[None, :] < atom_counts[:, None]).astype(jnp.float32).reshape(atom_num)
    hidden_t = (
        jnp.einsum("ic,ai->ca", msg_weight, features, preferred_element_type=jnp.float32)
        * mask_f[None, :]
    )
    own_pack = jnp.concatenate(
        [positions, hidden_t.astype(jnp.bfloat16).astype(jnp.float32)], axis=0
    )
    ext_pack = extended(own_pack, (("box", 1),), atom_num)
    pos_ext, hid_ext = ext_pack[:3], ext_pack[3:]

    def near_part(own, ext, feat_ext):
        return near_field(own, ext, feat_ext, pair_target, pair_source, pair_live)

    near_val, near_back = jax.vjp(near_part, positions, pos_ext, hid_ext)
    centers = jnp.repeat(leaf_centers, LEAF_ATOMS, axis=1)

    def far_basis(coords):
        return monomials((coords - centers) * REL_SCALE)

    basis_val, basis_back = jax.vjp(far_basis, positions)
    moment = jnp.einsum("ka,ca->kc", basis_val, hidden_t, precision=PRECISE)
    masked_feat = features.astype(jnp.float32) * mask_f[:, None]
    feat_basis = jnp.einsum("ka,ai->ki", basis_val, masked_feat, precision=PRECISE)
    counts_mat = jnp.sum(
        (far_list[:, :, None] == jnp.arange(groups, dtype=jnp.int32)[None, None, :]).astype(
            jnp.float32
        ),
        axis=1,
    )
    row_weights = lax.dynamic_index_in_dim(counts_mat, group_id, 0, keepdims=False)
    col_weights = lax.dynamic_index_in_dim(counts_mat, group_id, 1, keepdims=False)
    channels = moment.shape[1]
    subs = 8
    width = channels // subs
    rows = jnp.stack([moment, feat_basis]).reshape(2, -1, subs, width)
    moment_part = split_sum(rows.transpose(2, 0, 1, 3).reshape(-1), index, sub_bits[::-1])
    moment_tab = tree_gather(moment_part, index, grp_bits).reshape(groups, 2, -1, width)
    mixed_part = jnp.einsum("j,jnkc->nkc", row_weights, moment_tab, precision=PRECISE)
    gathered_part = mixed_part[0]
    local_part = jnp.dot(trans_weight, gathered_part, precision=PRECISE)
    both = tree_gather(jnp.stack([local_part, mixed_part[1]]).reshape(-1), index, sub_bits)
    both = both.reshape(subs, 2, -1, width).transpose(1, 2, 0, 3).reshape(2, -1, channels)
    local_exp, feat_mixed = both[0], both[1]
    potential = jnp.einsum("ka,kc->ac", basis_val, local_exp, precision=PRECISE)
    pre_act = near_val + potential
    sigma = jax.nn.sigmoid(pre_act)
    activ = pre_act * sigma
    atom_energy = mask_f * jnp.dot(activ, read_weight, precision=PRECISE)
    d_pre = mask_f[:, None] * read_weight[None, :] * (sigma + pre_act * sigma * (1.0 - sigma))
    grad_read_part = jnp.dot(mask_f, activ, precision=PRECISE)
    d_local = jnp.dot(basis_val, d_pre, precision=PRECISE)
    d_basis = jnp.einsum("kc,ac->ka", local_exp, d_pre, precision=PRECISE)
    d_rows = d_local.reshape(-1, subs, width).transpose(1, 0, 2).reshape(-1)
    d_local_part = split_sum(d_rows, index, sub_bits[::-1]).reshape(-1, width)
    grad_trans_part = jnp.einsum("kc,qc->kq", d_local_part, gathered_part, precision=PRECISE)
    d_gathered_part = jnp.dot(trans_weight.T, d_local_part, precision=PRECISE)
    slice_width = d_gathered_part.shape[1]
    far_msg_part = jnp.einsum("ki,kc->ic", feat_mixed, d_gathered_part, precision=PRECISE)
    far_msg = lax.dynamic_update_slice_in_dim(
        jnp.zeros((far_msg_part.shape[0], slice_width * 8), jnp.float32),
        far_msg_part,
        (index % 8) * slice_width,
        axis=1,
    )
    d_own, d_ext, d_feat_ext = near_back(d_pre)
    d_pack = jnp.concatenate([d_ext, d_feat_ext], axis=0)
    low_pack = passed_along(d_pack[:, :atom_num], "box", -1)
    high_pack = passed_along(d_pack[:, 2 * atom_num :], "box", 1)
    low_pos, low_feat = low_pack[:3], low_pack[3:]
    high_pos, high_feat = high_pack[:3], high_pack[3:]
    d_hidden_near = d_feat_ext[:, atom_num : 2 * atom_num] + low_feat + high_feat
    grad_msg_part = (
        jnp.einsum("ai,ca->ic", masked_feat, d_hidden_near, precision=PRECISE) + far_msg
    )
    flat = jnp.concatenate(
        [grad_msg_part.reshape(-1), grad_trans_part.reshape(-1), grad_read_part.reshape(-1)]
    )
    d_tab, flat = tree_gather_sum(d_gathered_part.reshape(-1), flat, index, grp_bits)
    d_tab = d_tab.reshape(groups, -1, width)
    d_moment_part = jnp.einsum("b,bkc->kc", col_weights, d_tab, precision=PRECISE)
    d_moment, flat = tree_gather_sum(d_moment_part.reshape(-1), flat, index, sub_bits)
    d_moment = d_moment.reshape(subs, -1, width).transpose(1, 0, 2).reshape(-1, channels)
    d_basis = d_basis + jnp.dot(d_moment, hidden_t, precision=PRECISE)
    (d_far_pos,) = basis_back(d_basis)
    msg_size, trans_size = grad_msg_part.size, grad_trans_part.size
    grad_msg = flat[:msg_size].reshape(grad_msg_part.shape)
    grad_trans = flat[msg_size : msg_size + trans_size].reshape(grad_trans_part.shape)
    grad_read = flat[msg_size + trans_size :]
    forces = -(d_own + d_ext[:, atom_num : 2 * atom_num] + low_pos + high_pos + d_far_pos)
    return (atom_energy, forces, grad_msg, grad_trans, grad_read)


def solution(mesh):
    return jax.shard_map(
        on_device,
        mesh=mesh,
        in_specs=(
            P(None, "box"),
            P(None, "box"),
            P("box"),
            P("box", None),
            P(),
            P(),
            P(),
            P("box"),
            P("box"),
            P("box"),
            P(),
        ),
        out_specs=(P("box"), P(None, "box"), P(), P(), P()),
        check_vma=False,
    )
```

```python
import jax
import jax.numpy as jnp
from jax import lax
from jax.sharding import PartitionSpec as P

LEAF_ATOMS = 64
PAIR_LEAF = 27


PRECISE = lax.Precision.HIGHEST
GAMMA = 3.0
NEAR_SCALE = 0.3
REL_SCALE = 0.5
EXPONENTS = [
    (power_x, power_y, degree - power_x - power_y)
    for degree in range(5)
    for power_x in range(degree, -1, -1)
    for power_y in range(degree - power_x, -1, -1)
]


def extended(block, sides, width):
    for axis, dim in sides:
        count = lax.axis_size(axis)
        forward = [(i, i + 1) for i in range(count - 1)]
        backward = [(target, source) for source, target in forward]
        low = lax.ppermute(
            lax.slice_in_dim(block, block.shape[dim] - width, None, axis=dim), axis, forward
        )
        high = lax.ppermute(lax.slice_in_dim(block, 0, width, axis=dim), axis, backward)
        block = jnp.concatenate([low, block, high], axis=dim)
    return block


def passed_along(block, axis, distance):
    devices = range(lax.axis_size(axis))
    route = [(i - distance, i) for i in devices if i - distance in devices]
    return lax.ppermute(block, axis, route)


def monomials(relative):
    powers = []
    for axis_id in range(3):
        coords = relative[axis_id]
        stacked = [jnp.ones_like(coords), coords]
        for degree in range(2, 5):
            stacked.append(stacked[-1] * coords)
        powers.append(stacked)
    return jnp.stack(
        [powers[0][ex_a] * powers[1][ex_b] * powers[2][ex_c] for ex_a, ex_b, ex_c in EXPONENTS]
    )


def near_field(pos_own, pos_ext, hid_ext, targets, sources, alive):
    leaves = pos_own.shape[1] // LEAF_ATOMS
    channels = hid_ext.shape[0]
    own_leaf = pos_own.reshape(3, leaves, LEAF_ATOMS)
    ext_leaf = pos_ext.reshape(3, 3 * leaves, LEAF_ATOMS)
    feat_leaf = hid_ext.reshape(channels, 3 * leaves, LEAF_ATOMS)
    tgt_hot = (targets[:, None] == jnp.arange(leaves, dtype=jnp.int32)[None, :]).astype(
        jnp.float32
    )
    src_hot = (sources[:, None] == jnp.arange(3 * leaves, dtype=jnp.int32)[None, :]).astype(
        jnp.float32
    )
    near_pos = jnp.einsum("pt,xti->xpi", tgt_hot, own_leaf, precision=PRECISE)
    far_pos = jnp.einsum("ps,xsj->xpj", src_hot, ext_leaf, precision=PRECISE)
    dist_sq = jnp.zeros((targets.shape[0], LEAF_ATOMS, LEAF_ATOMS), jnp.float32)
    for axis_id in range(3):
        offset_ax = near_pos[axis_id][:, :, None] - far_pos[axis_id][:, None, :]
        dist_sq = dist_sq + offset_ax * offset_ax
    kernel = (
        NEAR_SCALE * jnp.exp(-GAMMA * dist_sq) * alive.astype(jnp.float32)[:, None, None]
    ).astype(jnp.bfloat16)
    source_feat = jnp.einsum(
        "ps,csj->pjc", src_hot, feat_leaf, precision=lax.Precision.DEFAULT
    ).astype(jnp.bfloat16)
    contrib = jnp.einsum("pij,pjc->pic", kernel, source_feat, preferred_element_type=jnp.float32)
    accumulated = jnp.einsum("pt,pic->tic", tgt_hot, contrib, precision=lax.Precision.HIGH)
    return accumulated.reshape(leaves * LEAF_ATOMS, channels)


def xor_swap(block, bit):
    count = lax.axis_size("box")
    return lax.ppermute(block, "box", [(i, i ^ (1 << bit)) for i in range(count)])


def split_sum(block, index, bits):
    for bit in bits:
        half = block.shape[0] // 2
        lower, upper = block[:half], block[half:]
        up = ((index >> bit) & 1) == 1
        keep = jnp.where(up, upper, lower)
        send = jnp.where(up, lower, upper)
        block = keep + xor_swap(send, bit)
    return block


def tree_gather_sum(block, extra, index, bits):
    for bit in bits:
        packed = xor_swap(jnp.concatenate([block, extra]), bit)
        other, other_extra = packed[: block.size], packed[block.size :]
        up = ((index >> bit) & 1) == 1
        block = jnp.where(
            up, jnp.concatenate([other, block]), jnp.concatenate([block, other])
        )
        extra = extra + other_extra
    return block, extra


def tree_gather(block, index, bits):
    for bit in bits:
        other = xor_swap(block, bit)
        up = ((index >> bit) & 1) == 1
        block = jnp.where(
            up, jnp.concatenate([other, block]), jnp.concatenate([block, other])
        )
    return block


def on_device(
    positions,
    leaf_centers,
    atom_counts,
    features,
    msg_weight,
    trans_weight,
    read_weight,
    pair_target,
    pair_source,
    pair_live,
    far_list,
):
    atom_num = positions.shape[1]
    all_bits = lax.axis_size("box").bit_length() - 1
    sub_bits = tuple(range(3))
    grp_bits = tuple(range(3, all_bits))
    index = lax.axis_index("box")
    groups = lax.axis_size("box") // 8
    group_id = index // 8
    slot_ids = jnp.arange(LEAF_ATOMS, dtype=jnp.int32)
    mask_f = (slot_ids[None, :] < atom_counts[:, None]).astype(jnp.float32).reshape(atom_num)
    hidden_t = (
        jnp.einsum("ic,ai->ca", msg_weight, features, preferred_element_type=jnp.float32)
        * mask_f[None, :]
    )
    own_pack = jnp.concatenate(
        [positions, hidden_t.astype(jnp.bfloat16).astype(jnp.float32)], axis=0
    )
    ext_pack = extended(own_pack, (("box", 1),), atom_num)
    pos_ext, hid_ext = ext_pack[:3], ext_pack[3:]

    def near_part(own, ext, feat_ext):
        return near_field(own, ext, feat_ext, pair_target, pair_source, pair_live)

    near_val, near_back = jax.vjp(near_part, positions, pos_ext, hid_ext)
    centers = jnp.repeat(leaf_centers, LEAF_ATOMS, axis=1)

    def far_basis(coords):
        return monomials((coords - centers) * REL_SCALE)

    basis_val, basis_back = jax.vjp(far_basis, positions)
    moment = jnp.einsum("ka,ca->kc", basis_val, hidden_t, precision=PRECISE)
    masked_feat = features.astype(jnp.float32) * mask_f[:, None]
    feat_basis = jnp.einsum("ka,ai->ki", basis_val, masked_feat, precision=PRECISE)
    counts_mat = jnp.sum(
        (far_list[:, :, None] == jnp.arange(groups, dtype=jnp.int32)[None, None, :]).astype(
            jnp.float32
        ),
        axis=1,
    )
    row_weights = lax.dynamic_index_in_dim(counts_mat, group_id, 0, keepdims=False)
    col_weights = lax.dynamic_index_in_dim(counts_mat, group_id, 1, keepdims=False)
    channels = moment.shape[1]
    subs = 8
    width = channels // subs
    rows = jnp.stack([moment, feat_basis]).reshape(2, -1, subs, width)
    moment_part = split_sum(rows.transpose(2, 0, 1, 3).reshape(-1), index, sub_bits[::-1])
    moment_tab = tree_gather(moment_part, index, grp_bits).reshape(groups, 2, -1, width)
    mixed_part = jnp.einsum("j,jnkc->nkc", row_weights, moment_tab, precision=PRECISE)
    gathered_part = mixed_part[0]
    local_part = jnp.dot(trans_weight, gathered_part, precision=PRECISE)
    both = tree_gather(jnp.stack([local_part, mixed_part[1]]).reshape(-1), index, sub_bits)
    both = both.reshape(subs, 2, -1, width).transpose(1, 2, 0, 3).reshape(2, -1, channels)
    local_exp, feat_mixed = both[0], both[1]
    potential = jnp.einsum("ka,kc->ac", basis_val, local_exp, precision=PRECISE)
    pre_act = near_val + potential
    sigma = jax.nn.sigmoid(pre_act)
    activ = pre_act * sigma
    atom_energy = mask_f * jnp.dot(activ, read_weight, precision=PRECISE)
    d_pre = mask_f[:, None] * read_weight[None, :] * (sigma + pre_act * sigma * (1.0 - sigma))
    grad_read_part = jnp.dot(mask_f, activ, precision=PRECISE)
    d_local = jnp.dot(basis_val, d_pre, precision=PRECISE)
    d_basis = jnp.einsum("kc,ac->ka", local_exp, d_pre, precision=PRECISE)
    d_rows = d_local.reshape(-1, subs, width).transpose(1, 0, 2).reshape(-1)
    d_local_part = split_sum(d_rows, index, sub_bits[::-1]).reshape(-1, width)
    grad_trans_part = jnp.einsum("kc,qc->kq", d_local_part, gathered_part, precision=PRECISE)
    d_gathered_part = jnp.dot(trans_weight.T, d_local_part, precision=PRECISE)
    slice_width = d_gathered_part.shape[1]
    far_msg_part = jnp.einsum("ki,kc->ic", feat_mixed, d_gathered_part, precision=PRECISE)
    far_msg = lax.dynamic_update_slice_in_dim(
        jnp.zeros((far_msg_part.shape[0], slice_width * 8), jnp.float32),
        far_msg_part,
        (index % 8) * slice_width,
        axis=1,
    )
    d_own, d_ext, d_feat_ext = near_back(d_pre)
    d_pack = jnp.concatenate([d_ext, d_feat_ext], axis=0)
    low_pack = passed_along(d_pack[:, :atom_num], "box", -1)
    high_pack = passed_along(d_pack[:, 2 * atom_num :], "box", 1)
    low_pos, low_feat = low_pack[:3], low_pack[3:]
    high_pos, high_feat = high_pack[:3], high_pack[3:]
    d_hidden_near = d_feat_ext[:, atom_num : 2 * atom_num] + low_feat + high_feat
    grad_msg_part = (
        jnp.einsum("ai,ca->ic", masked_feat, d_hidden_near, precision=PRECISE) + far_msg
    )
    flat = jnp.concatenate(
        [grad_msg_part.reshape(-1), grad_trans_part.reshape(-1), grad_read_part.reshape(-1)]
    )
    d_tab, flat = tree_gather_sum(d_gathered_part.reshape(-1), flat, index, grp_bits)
    d_tab = d_tab.reshape(groups, -1, width)
    d_moment_part = jnp.einsum("b,bkc->kc", col_weights, d_tab, precision=PRECISE)
    d_moment, flat = tree_gather_sum(d_moment_part.reshape(-1), flat, index, sub_bits)
    d_moment = d_moment.reshape(subs, -1, width).transpose(1, 0, 2).reshape(-1, channels)
    d_basis = d_basis + jnp.dot(d_moment, hidden_t, precision=PRECISE)
    (d_far_pos,) = basis_back(d_basis)
    msg_size, trans_size = grad_msg_part.size, grad_trans_part.size
    grad_msg = flat[:msg_size].reshape(grad_msg_part.shape)
    grad_trans = flat[msg_size : msg_size + trans_size].reshape(grad_trans_part.shape)
    grad_read = flat[msg_size + trans_size :]
    forces = -(d_own + d_ext[:, atom_num : 2 * atom_num] + low_pos + high_pos + d_far_pos)
    return (atom_energy, forces, grad_msg, grad_trans, grad_read)


def solution(mesh):
    return jax.shard_map(
        on_device,
        mesh=mesh,
        in_specs=(
            P(None, "box"),
            P(None, "box"),
            P("box"),
            P("box", None),
            P(),
            P(),
            P(),
            P("box"),
            P("box"),
            P("box"),
            P(),
        ),
        out_specs=(P("box"), P(None, "box"), P(), P(), P()),
        check_vma=False,
    )
```

```python
import jax
import jax.numpy as jnp
from jax import lax
from jax.sharding import PartitionSpec as P

LEAF_ATOMS = 64
PAIR_LEAF = 27


PRECISE = lax.Precision.HIGHEST
GAMMA = 3.0
NEAR_SCALE = 0.3
REL_SCALE = 0.5
EXPONENTS = [
    (power_x, power_y, degree - power_x - power_y)
    for degree in range(5)
    for power_x in range(degree, -1, -1)
    for power_y in range(degree - power_x, -1, -1)
]


def extended(block, sides, width):
    for axis, dim in sides:
        count = lax.axis_size(axis)
        forward = [(i, i + 1) for i in range(count - 1)]
        backward = [(target, source) for source, target in forward]
        low = lax.ppermute(
            lax.slice_in_dim(block, block.shape[dim] - width, None, axis=dim), axis, forward
        )
        high = lax.ppermute(lax.slice_in_dim(block, 0, width, axis=dim), axis, backward)
        block = jnp.concatenate([low, block, high], axis=dim)
    return block


def passed_along(block, axis, distance):
    devices = range(lax.axis_size(axis))
    route = [(i - distance, i) for i in devices if i - distance in devices]
    return lax.ppermute(block, axis, route)


def monomials(relative):
    powers = []
    for axis_id in range(3):
        coords = relative[axis_id]
        stacked = [jnp.ones_like(coords), coords]
        for degree in range(2, 5):
            stacked.append(stacked[-1] * coords)
        powers.append(stacked)
    return jnp.stack(
        [powers[0][ex_a] * powers[1][ex_b] * powers[2][ex_c] for ex_a, ex_b, ex_c in EXPONENTS]
    )


def near_field(pos_own, pos_ext, hid_ext, targets, sources, alive):
    leaves = pos_own.shape[1] // LEAF_ATOMS
    channels = hid_ext.shape[0]
    own_leaf = pos_own.reshape(3, leaves, LEAF_ATOMS)
    ext_leaf = pos_ext.reshape(3, 3 * leaves, LEAF_ATOMS)
    feat_leaf = hid_ext.reshape(channels, 3 * leaves, LEAF_ATOMS)
    tgt_hot = (targets[:, None] == jnp.arange(leaves, dtype=jnp.int32)[None, :]).astype(
        jnp.float32
    )
    src_hot = (sources[:, None] == jnp.arange(3 * leaves, dtype=jnp.int32)[None, :]).astype(
        jnp.float32
    )
    near_pos = jnp.einsum("pt,xti->xpi", tgt_hot, own_leaf, precision=PRECISE)
    far_pos = jnp.einsum("ps,xsj->xpj", src_hot, ext_leaf, precision=PRECISE)
    dist_sq = jnp.zeros((targets.shape[0], LEAF_ATOMS, LEAF_ATOMS), jnp.float32)
    for axis_id in range(3):
        offset_ax = near_pos[axis_id][:, :, None] - far_pos[axis_id][:, None, :]
        dist_sq = dist_sq + offset_ax * offset_ax
    kernel = (
        NEAR_SCALE * jnp.exp(-GAMMA * dist_sq) * alive.astype(jnp.float32)[:, None, None]
    ).astype(jnp.bfloat16)
    source_feat = jnp.einsum(
        "ps,csj->pjc", src_hot, feat_leaf, precision=lax.Precision.DEFAULT
    ).astype(jnp.bfloat16)
    contrib = jnp.einsum("pij,pjc->pic", kernel, source_feat, preferred_element_type=jnp.float32)
    accumulated = jnp.einsum("pt,pic->tic", tgt_hot, contrib, precision=lax.Precision.HIGH)
    return accumulated.reshape(leaves * LEAF_ATOMS, channels)


def xor_swap(block, bit):
    count = lax.axis_size("box")
    return lax.ppermute(block, "box", [(i, i ^ (1 << bit)) for i in range(count)])


def split_sum(block, index, bits):
    for bit in bits:
        half = block.shape[0] // 2
        lower, upper = block[:half], block[half:]
        up = ((index >> bit) & 1) == 1
        keep = jnp.where(up, upper, lower)
        send = jnp.where(up, lower, upper)
        block = keep + xor_swap(send, bit)
    return block


def tree_gather_sum(block, extra, index, bits):
    for bit in bits:
        packed = xor_swap(jnp.concatenate([block, extra]), bit)
        other, other_extra = packed[: block.size], packed[block.size :]
        up = ((index >> bit) & 1) == 1
        block = jnp.where(
            up, jnp.concatenate([other, block]), jnp.concatenate([block, other])
        )
        extra = extra + other_extra
    return block, extra


def tree_gather(block, index, bits):
    for bit in bits:
        other = xor_swap(block, bit)
        up = ((index >> bit) & 1) == 1
        block = jnp.where(
            up, jnp.concatenate([other, block]), jnp.concatenate([block, other])
        )
    return block


def on_device(
    positions,
    leaf_centers,
    atom_counts,
    features,
    msg_weight,
    trans_weight,
    read_weight,
    pair_target,
    pair_source,
    pair_live,
    far_list,
):
    atom_num = positions.shape[1]
    all_bits = lax.axis_size("box").bit_length() - 1
    sub_bits = tuple(range(3))
    grp_bits = tuple(range(3, all_bits))
    index = lax.axis_index("box")
    groups = lax.axis_size("box") // 8
    group_id = index // 8
    slot_ids = jnp.arange(LEAF_ATOMS, dtype=jnp.int32)
    mask_f = (slot_ids[None, :] < atom_counts[:, None]).astype(jnp.float32).reshape(atom_num)
    hidden_t = (
        jnp.einsum("ic,ai->ca", msg_weight, features, preferred_element_type=jnp.float32)
        * mask_f[None, :]
    )
    masked_feat = features.astype(jnp.float32) * mask_f[:, None]
    channels = hidden_t.shape[0]
    own_pack = jnp.concatenate(
        [positions, hidden_t.astype(jnp.bfloat16).astype(jnp.float32), masked_feat.T], axis=0
    )
    ext_pack = extended(own_pack, (("box", 1),), atom_num)
    pos_ext, hid_ext = ext_pack[:3], ext_pack[3 : 3 + channels]
    feat_ext = ext_pack[3 + channels :]

    def near_part(own, ext, feat_ext):
        return near_field(own, ext, feat_ext, pair_target, pair_source, pair_live)

    near_val, near_back = jax.vjp(near_part, positions, pos_ext, hid_ext)
    centers = jnp.repeat(leaf_centers, LEAF_ATOMS, axis=1)

    def far_basis(coords):
        return monomials((coords - centers) * REL_SCALE)

    basis_val, basis_back = jax.vjp(far_basis, positions)
    moment = jnp.einsum("ka,ca->kc", basis_val, hidden_t, precision=PRECISE)
    feat_basis = jnp.einsum("ka,ai->ki", basis_val, masked_feat, precision=PRECISE)
    counts_mat = jnp.sum(
        (far_list[:, :, None] == jnp.arange(groups, dtype=jnp.int32)[None, None, :]).astype(
            jnp.float32
        ),
        axis=1,
    )
    row_weights = lax.dynamic_index_in_dim(counts_mat, group_id, 0, keepdims=False)
    col_weights = lax.dynamic_index_in_dim(counts_mat, group_id, 1, keepdims=False)
    subs = 8
    width = channels // subs
    rows = jnp.stack([moment, feat_basis]).reshape(2, -1, subs, width)
    moment_part = split_sum(rows.transpose(2, 0, 1, 3).reshape(-1), index, sub_bits[::-1])
    moment_tab = tree_gather(moment_part, index, grp_bits).reshape(groups, 2, -1, width)
    mixed_part = jnp.einsum("j,jnkc->nkc", row_weights, moment_tab, precision=PRECISE)
    gathered_part = mixed_part[0]
    local_part = jnp.dot(trans_weight, gathered_part, precision=PRECISE)
    both = tree_gather(jnp.stack([local_part, mixed_part[1]]).reshape(-1), index, sub_bits)
    both = both.reshape(subs, 2, -1, width).transpose(1, 2, 0, 3).reshape(2, -1, channels)
    local_exp, feat_mixed = both[0], both[1]
    potential = jnp.einsum("ka,kc->ac", basis_val, local_exp, precision=PRECISE)
    pre_act = near_val + potential
    sigma = jax.nn.sigmoid(pre_act)
    activ = pre_act * sigma
    atom_energy = mask_f * jnp.dot(activ, read_weight, precision=PRECISE)
    d_pre = mask_f[:, None] * read_weight[None, :] * (sigma + pre_act * sigma * (1.0 - sigma))
    grad_read_part = jnp.dot(mask_f, activ, precision=PRECISE)
    d_local = jnp.dot(basis_val, d_pre, precision=PRECISE)
    d_basis = jnp.einsum("kc,ac->ka", local_exp, d_pre, precision=PRECISE)
    d_rows = d_local.reshape(-1, subs, width).transpose(1, 0, 2).reshape(-1)
    d_local_part = split_sum(d_rows, index, sub_bits[::-1]).reshape(-1, width)
    grad_trans_part = jnp.einsum("kc,qc->kq", d_local_part, gathered_part, precision=PRECISE)
    d_gathered_part = jnp.dot(trans_weight.T, d_local_part, precision=PRECISE)
    slice_width = d_gathered_part.shape[1]
    far_msg_part = jnp.einsum("ki,kc->ic", feat_mixed, d_gathered_part, precision=PRECISE)
    far_msg = lax.dynamic_update_slice_in_dim(
        jnp.zeros((far_msg_part.shape[0], slice_width * 8), jnp.float32),
        far_msg_part,
        (index % 8) * slice_width,
        axis=1,
    )
    d_own, d_ext, d_feat_ext = near_back(d_pre)
    low_pos = passed_along(d_ext[:, :atom_num], "box", -1)
    high_pos = passed_along(d_ext[:, 2 * atom_num :], "box", 1)
    grad_msg_part = (
        jnp.einsum("ia,ca->ic", feat_ext, d_feat_ext, precision=PRECISE) + far_msg
    )
    flat = jnp.concatenate(
        [grad_msg_part.reshape(-1), grad_trans_part.reshape(-1), grad_read_part.reshape(-1)]
    )
    d_tab, flat = tree_gather_sum(d_gathered_part.reshape(-1), flat, index, grp_bits)
    d_tab = d_tab.reshape(groups, -1, width)
    d_moment_part = jnp.einsum("b,bkc->kc", col_weights, d_tab, precision=PRECISE)
    d_moment, flat = tree_gather_sum(d_moment_part.reshape(-1), flat, index, sub_bits)
    d_moment = d_moment.reshape(subs, -1, width).transpose(1, 0, 2).reshape(-1, channels)
    d_basis = d_basis + jnp.dot(d_moment, hidden_t, precision=PRECISE)
    (d_far_pos,) = basis_back(d_basis)
    msg_size, trans_size = grad_msg_part.size, grad_trans_part.size
    grad_msg = flat[:msg_size].reshape(grad_msg_part.shape)
    grad_trans = flat[msg_size : msg_size + trans_size].reshape(grad_trans_part.shape)
    grad_read = flat[msg_size + trans_size :]
    forces = -(d_own + d_ext[:, atom_num : 2 * atom_num] + low_pos + high_pos + d_far_pos)
    return (atom_energy, forces, grad_msg, grad_trans, grad_read)


def solution(mesh):
    return jax.shard_map(
        on_device,
        mesh=mesh,
        in_specs=(
            P(None, "box"),
            P(None, "box"),
            P("box"),
            P("box", None),
            P(),
            P(),
            P(),
            P("box"),
            P("box"),
            P("box"),
            P(),
        ),
        out_specs=(P("box"), P(None, "box"), P(), P(), P()),
        check_vma=False,
    )
```

```python
import jax
import jax.numpy as jnp
from jax import lax
from jax.sharding import PartitionSpec as P

LEAF_ATOMS = 64
PAIR_LEAF = 27


PRECISE = lax.Precision.HIGHEST
GAMMA = 3.0
NEAR_SCALE = 0.3
REL_SCALE = 0.5
EXPONENTS = [
    (power_x, power_y, degree - power_x - power_y)
    for degree in range(5)
    for power_x in range(degree, -1, -1)
    for power_y in range(degree - power_x, -1, -1)
]


def extended(block, sides, width):
    for axis, dim in sides:
        count = lax.axis_size(axis)
        forward = [(i, i + 1) for i in range(count - 1)]
        backward = [(target, source) for source, target in forward]
        low = lax.ppermute(
            lax.slice_in_dim(block, block.shape[dim] - width, None, axis=dim), axis, forward
        )
        high = lax.ppermute(lax.slice_in_dim(block, 0, width, axis=dim), axis, backward)
        block = jnp.concatenate([low, block, high], axis=dim)
    return block


def passed_along(block, axis, distance):
    devices = range(lax.axis_size(axis))
    route = [(i - distance, i) for i in devices if i - distance in devices]
    return lax.ppermute(block, axis, route)


def monomials(relative):
    powers = []
    for axis_id in range(3):
        coords = relative[axis_id]
        stacked = [jnp.ones_like(coords), coords]
        for degree in range(2, 5):
            stacked.append(stacked[-1] * coords)
        powers.append(stacked)
    return jnp.stack(
        [powers[0][ex_a] * powers[1][ex_b] * powers[2][ex_c] for ex_a, ex_b, ex_c in EXPONENTS]
    )


def near_field(pos_own, pos_ext, hid_ext, targets, sources, alive):
    leaves = pos_own.shape[1] // LEAF_ATOMS
    channels = hid_ext.shape[0]
    own_leaf = pos_own.reshape(3, leaves, LEAF_ATOMS)
    ext_leaf = pos_ext.reshape(3, 3 * leaves, LEAF_ATOMS)
    feat_leaf = hid_ext.reshape(channels, 3 * leaves, LEAF_ATOMS)
    tgt_hot = (targets[:, None] == jnp.arange(leaves, dtype=jnp.int32)[None, :]).astype(
        jnp.float32
    )
    src_hot = (sources[:, None] == jnp.arange(3 * leaves, dtype=jnp.int32)[None, :]).astype(
        jnp.float32
    )
    near_pos = jnp.einsum("pt,xti->xpi", tgt_hot, own_leaf, precision=PRECISE)
    far_pos = jnp.einsum("ps,xsj->xpj", src_hot, ext_leaf, precision=PRECISE)
    dist_sq = jnp.zeros((targets.shape[0], LEAF_ATOMS, LEAF_ATOMS), jnp.float32)
    for axis_id in range(3):
        offset_ax = near_pos[axis_id][:, :, None] - far_pos[axis_id][:, None, :]
        dist_sq = dist_sq + offset_ax * offset_ax
    kernel = (
        NEAR_SCALE * jnp.exp(-GAMMA * dist_sq) * alive.astype(jnp.float32)[:, None, None]
    ).astype(jnp.bfloat16)
    source_feat = jnp.einsum(
        "ps,csj->pjc", src_hot, feat_leaf, precision=lax.Precision.DEFAULT
    ).astype(jnp.bfloat16)
    contrib = jnp.einsum("pij,pjc->pic", kernel, source_feat, preferred_element_type=jnp.float32)
    accumulated = jnp.einsum("pt,pic->tic", tgt_hot, contrib, precision=lax.Precision.HIGH)
    return accumulated.reshape(leaves * LEAF_ATOMS, channels)


def xor_swap(block, bit):
    count = lax.axis_size("box")
    return lax.ppermute(block, "box", [(i, i ^ (1 << bit)) for i in range(count)])


def split_sum(block, index, bits):
    for bit in bits:
        half = block.shape[0] // 2
        lower, upper = block[:half], block[half:]
        up = ((index >> bit) & 1) == 1
        keep = jnp.where(up, upper, lower)
        send = jnp.where(up, lower, upper)
        block = keep + xor_swap(send, bit)
    return block


def tree_gather_sum(block, extra, index, bits):
    for bit in bits:
        packed = xor_swap(jnp.concatenate([block, extra]), bit)
        other, other_extra = packed[: block.size], packed[block.size :]
        up = ((index >> bit) & 1) == 1
        block = jnp.where(
            up, jnp.concatenate([other, block]), jnp.concatenate([block, other])
        )
        extra = extra + other_extra
    return block, extra


def tree_gather(block, index, bits):
    for bit in bits:
        other = xor_swap(block, bit)
        up = ((index >> bit) & 1) == 1
        block = jnp.where(
            up, jnp.concatenate([other, block]), jnp.concatenate([block, other])
        )
    return block


def on_device(
    positions,
    leaf_centers,
    atom_counts,
    features,
    msg_weight,
    trans_weight,
    read_weight,
    pair_target,
    pair_source,
    pair_live,
    far_list,
):
    atom_num = positions.shape[1]
    all_bits = lax.axis_size("box").bit_length() - 1
    sub_bits = tuple(range(3))
    grp_bits = tuple(range(3, all_bits))
    index = lax.axis_index("box")
    groups = lax.axis_size("box") // 8
    group_id = index // 8
    slot_ids = jnp.arange(LEAF_ATOMS, dtype=jnp.int32)
    mask_f = (slot_ids[None, :] < atom_counts[:, None]).astype(jnp.float32).reshape(atom_num)
    hidden_t = (
        jnp.einsum("ic,ai->ca", msg_weight, features, preferred_element_type=jnp.float32)
        * mask_f[None, :]
    )
    own_pack = jnp.concatenate(
        [positions, hidden_t.astype(jnp.bfloat16).astype(jnp.float32)], axis=0
    )
    ext_pack = extended(own_pack, (("box", 1),), atom_num)
    pos_ext, hid_ext = ext_pack[:3], ext_pack[3:]

    def near_part(own, ext, feat_ext):
        return near_field(own, ext, feat_ext, pair_target, pair_source, pair_live)

    near_val, near_back = jax.vjp(near_part, positions, pos_ext, hid_ext)
    centers = jnp.repeat(leaf_centers, LEAF_ATOMS, axis=1)

    def far_basis(coords):
        return monomials((coords - centers) * REL_SCALE)

    basis_val, basis_back = jax.vjp(far_basis, positions)
    moment = jnp.einsum("ka,ca->kc", basis_val, hidden_t, precision=PRECISE)
    masked_feat = features.astype(jnp.float32) * mask_f[:, None]
    feat_basis = jnp.einsum("ka,ai->ki", basis_val, masked_feat, precision=PRECISE)
    counts_mat = jnp.sum(
        (far_list[:, :, None] == jnp.arange(groups, dtype=jnp.int32)[None, None, :]).astype(
            jnp.float32
        ),
        axis=1,
    )
    row_weights = lax.dynamic_index_in_dim(counts_mat, group_id, 0, keepdims=False)
    col_weights = lax.dynamic_index_in_dim(counts_mat, group_id, 1, keepdims=False)
    channels = moment.shape[1]
    subs = 8
    width = channels // subs
    rows = jnp.stack([moment, feat_basis]).reshape(2, -1, subs, width)
    moment_part = split_sum(rows.transpose(2, 0, 1, 3).reshape(-1), index, sub_bits[::-1])
    moment_tab = tree_gather(moment_part, index, grp_bits).reshape(groups, 2, -1, width)
    mixed_part = jnp.einsum("j,jnkc->nkc", row_weights, moment_tab, precision=PRECISE)
    gathered_part = mixed_part[0]
    local_part = jnp.dot(trans_weight, gathered_part, precision=PRECISE)
    both = tree_gather(jnp.stack([local_part, mixed_part[1]]).reshape(-1), index, sub_bits)
    both = both.reshape(subs, 2, -1, width).transpose(1, 2, 0, 3).reshape(2, -1, channels)
    local_exp, feat_mixed = both[0], both[1]
    potential = jnp.einsum("ka,kc->ac", basis_val, local_exp, precision=PRECISE)
    pre_act = near_val + potential
    sigma = jax.nn.sigmoid(pre_act)
    activ = pre_act * sigma
    atom_energy = mask_f * jnp.dot(activ, read_weight, precision=PRECISE)
    d_pre = mask_f[:, None] * read_weight[None, :] * (sigma + pre_act * sigma * (1.0 - sigma))
    grad_read_part = jnp.dot(mask_f, activ, precision=PRECISE)
    d_local = jnp.dot(basis_val, d_pre, precision=PRECISE)
    d_basis = jnp.einsum("kc,ac->ka", local_exp, d_pre, precision=PRECISE)
    d_rows = d_local.reshape(-1, subs, width).transpose(1, 0, 2).reshape(-1)
    d_local_part = split_sum(d_rows, index, sub_bits[::-1]).reshape(-1, width)
    grad_trans_part = jnp.einsum("kc,qc->kq", d_local_part, gathered_part, precision=PRECISE)
    d_gathered_part = jnp.dot(trans_weight.T, d_local_part, precision=PRECISE)
    slice_width = d_gathered_part.shape[1]
    far_msg_part = jnp.einsum("ki,kc->ic", feat_mixed, d_gathered_part, precision=PRECISE)
    far_msg = lax.dynamic_update_slice_in_dim(
        jnp.zeros((far_msg_part.shape[0], slice_width * 8), jnp.float32),
        far_msg_part,
        (index % 8) * slice_width,
        axis=1,
    )
    d_own, d_ext, d_feat_ext = near_back(d_pre)
    d_pack = jnp.concatenate([d_ext, d_feat_ext], axis=0)
    low_pack = passed_along(d_pack[:, :atom_num], "box", -1)
    high_pack = passed_along(d_pack[:, 2 * atom_num :].astype(jnp.bfloat16), "box", 1).astype(
        jnp.float32
    )
    low_pos, low_feat = low_pack[:3], low_pack[3:]
    high_pos, high_feat = high_pack[:3], high_pack[3:]
    d_hidden_near = d_feat_ext[:, atom_num : 2 * atom_num] + low_feat + high_feat
    grad_msg_part = (
        jnp.einsum("ai,ca->ic", masked_feat, d_hidden_near, precision=PRECISE) + far_msg
    )
    flat = jnp.concatenate(
        [grad_msg_part.reshape(-1), grad_trans_part.reshape(-1), grad_read_part.reshape(-1)]
    )
    d_tab, flat = tree_gather_sum(d_gathered_part.reshape(-1), flat, index, grp_bits)
    d_tab = d_tab.reshape(groups, -1, width)
    d_moment_part = jnp.einsum("b,bkc->kc", col_weights, d_tab, precision=PRECISE)
    d_moment, flat = tree_gather_sum(d_moment_part.reshape(-1), flat, index, sub_bits)
    d_moment = d_moment.reshape(subs, -1, width).transpose(1, 0, 2).reshape(-1, channels)
    d_basis = d_basis + jnp.dot(d_moment, hidden_t, precision=PRECISE)
    (d_far_pos,) = basis_back(d_basis)
    msg_size, trans_size = grad_msg_part.size, grad_trans_part.size
    grad_msg = flat[:msg_size].reshape(grad_msg_part.shape)
    grad_trans = flat[msg_size : msg_size + trans_size].reshape(grad_trans_part.shape)
    grad_read = flat[msg_size + trans_size :]
    forces = -(d_own + d_ext[:, atom_num : 2 * atom_num] + low_pos + high_pos + d_far_pos)
    return (atom_energy, forces, grad_msg, grad_trans, grad_read)


def solution(mesh):
    return jax.shard_map(
        on_device,
        mesh=mesh,
        in_specs=(
            P(None, "box"),
            P(None, "box"),
            P("box"),
            P("box", None),
            P(),
            P(),
            P(),
            P("box"),
            P("box"),
            P("box"),
            P(),
        ),
        out_specs=(P("box"), P(None, "box"), P(), P(), P()),
        check_vma=False,
    )
```

```python
import jax
import jax.numpy as jnp
from jax import lax
from jax.sharding import PartitionSpec as P

LEAF_ATOMS = 64
PAIR_LEAF = 27


PRECISE = lax.Precision.HIGHEST
GAMMA = 3.0
NEAR_SCALE = 0.3
REL_SCALE = 0.5
EXPONENTS = [
    (power_x, power_y, degree - power_x - power_y)
    for degree in range(5)
    for power_x in range(degree, -1, -1)
    for power_y in range(degree - power_x, -1, -1)
]


def extended(block, sides, width):
    for axis, dim in sides:
        count = lax.axis_size(axis)
        forward = [(i, i + 1) for i in range(count - 1)]
        backward = [(target, source) for source, target in forward]
        low = lax.ppermute(
            lax.slice_in_dim(block, block.shape[dim] - width, None, axis=dim), axis, forward
        )
        high = lax.ppermute(lax.slice_in_dim(block, 0, width, axis=dim), axis, backward)
        block = jnp.concatenate([low, block, high], axis=dim)
    return block


def passed_along(block, axis, distance):
    devices = range(lax.axis_size(axis))
    route = [(i - distance, i) for i in devices if i - distance in devices]
    return lax.ppermute(block, axis, route)


def monomials(relative):
    powers = []
    for axis_id in range(3):
        coords = relative[axis_id]
        stacked = [jnp.ones_like(coords), coords]
        for degree in range(2, 5):
            stacked.append(stacked[-1] * coords)
        powers.append(stacked)
    return jnp.stack(
        [powers[0][ex_a] * powers[1][ex_b] * powers[2][ex_c] for ex_a, ex_b, ex_c in EXPONENTS]
    )


def near_field(pos_own, pos_ext, hid_ext, targets, sources, alive):
    leaves = pos_own.shape[1] // LEAF_ATOMS
    channels = hid_ext.shape[0]
    own_leaf = pos_own.reshape(3, leaves, LEAF_ATOMS)
    ext_leaf = pos_ext.reshape(3, 3 * leaves, LEAF_ATOMS)
    feat_leaf = hid_ext.reshape(channels, 3 * leaves, LEAF_ATOMS)
    tgt_hot = (targets[:, None] == jnp.arange(leaves, dtype=jnp.int32)[None, :]).astype(
        jnp.float32
    )
    src_hot = (sources[:, None] == jnp.arange(3 * leaves, dtype=jnp.int32)[None, :]).astype(
        jnp.float32
    )
    near_pos = jnp.einsum("pt,xti->xpi", tgt_hot, own_leaf, precision=PRECISE)
    far_pos = jnp.einsum("ps,xsj->xpj", src_hot, ext_leaf, precision=PRECISE)
    dist_sq = jnp.zeros((targets.shape[0], LEAF_ATOMS, LEAF_ATOMS), jnp.float32)
    for axis_id in range(3):
        offset_ax = near_pos[axis_id][:, :, None] - far_pos[axis_id][:, None, :]
        dist_sq = dist_sq + offset_ax * offset_ax
    kernel = (
        NEAR_SCALE * jnp.exp(-GAMMA * dist_sq) * alive.astype(jnp.float32)[:, None, None]
    ).astype(jnp.bfloat16)
    source_feat = jnp.einsum(
        "ps,csj->pjc", src_hot, feat_leaf, precision=lax.Precision.DEFAULT
    ).astype(jnp.bfloat16)
    contrib = jnp.einsum("pij,pjc->pic", kernel, source_feat, preferred_element_type=jnp.float32)
    accumulated = jnp.einsum("pt,pic->tic", tgt_hot, contrib, precision=lax.Precision.HIGH)
    return accumulated.reshape(leaves * LEAF_ATOMS, channels)


def xor_swap(block, bit):
    count = lax.axis_size("box")
    return lax.ppermute(block, "box", [(i, i ^ (1 << bit)) for i in range(count)])


def split_sum(block, index, bits):
    for bit in bits:
        half = block.shape[0] // 2
        lower, upper = block[:half], block[half:]
        up = ((index >> bit) & 1) == 1
        keep = jnp.where(up, upper, lower)
        send = jnp.where(up, lower, upper)
        block = keep + xor_swap(send, bit)
    return block


def tree_gather_sum(block, extra, index, bits):
    for bit in bits:
        packed = xor_swap(jnp.concatenate([block, extra]), bit)
        other, other_extra = packed[: block.size], packed[block.size :]
        up = ((index >> bit) & 1) == 1
        block = jnp.where(
            up, jnp.concatenate([other, block]), jnp.concatenate([block, other])
        )
        extra = extra + other_extra
    return block, extra


def tree_gather(block, index, bits):
    for bit in bits:
        other = xor_swap(block, bit)
        up = ((index >> bit) & 1) == 1
        block = jnp.where(
            up, jnp.concatenate([other, block]), jnp.concatenate([block, other])
        )
    return block


def on_device(
    positions,
    leaf_centers,
    atom_counts,
    features,
    msg_weight,
    trans_weight,
    read_weight,
    pair_target,
    pair_source,
    pair_live,
    far_list,
):
    atom_num = positions.shape[1]
    all_bits = lax.axis_size("box").bit_length() - 1
    sub_bits = tuple(range(3))
    grp_bits = tuple(range(3, all_bits))
    index = lax.axis_index("box")
    groups = lax.axis_size("box") // 8
    group_id = index // 8
    slot_ids = jnp.arange(LEAF_ATOMS, dtype=jnp.int32)
    mask_f = (slot_ids[None, :] < atom_counts[:, None]).astype(jnp.float32).reshape(atom_num)
    hidden_t = (
        jnp.einsum("ic,ai->ca", msg_weight, features, preferred_element_type=jnp.float32)
        * mask_f[None, :]
    )
    own_pack = jnp.concatenate(
        [positions, hidden_t.astype(jnp.bfloat16).astype(jnp.float32)], axis=0
    )
    ext_pack = extended(own_pack, (("box", 1),), atom_num)
    pos_ext, hid_ext = ext_pack[:3], ext_pack[3:]

    def near_part(own, ext, feat_ext):
        return near_field(own, ext, feat_ext, pair_target, pair_source, pair_live)

    near_val, near_back = jax.vjp(near_part, positions, pos_ext, hid_ext)
    centers = jnp.repeat(leaf_centers, LEAF_ATOMS, axis=1)

    def far_basis(coords):
        return monomials((coords - centers) * REL_SCALE)

    basis_val, basis_back = jax.vjp(far_basis, positions)
    moment = jnp.einsum("ka,ca->kc", basis_val, hidden_t, precision=PRECISE)
    masked_feat = features.astype(jnp.float32) * mask_f[:, None]
    feat_basis = jnp.einsum("ka,ai->ki", basis_val, masked_feat, precision=PRECISE)
    counts_mat = jnp.sum(
        (far_list[:, :, None] == jnp.arange(groups, dtype=jnp.int32)[None, None, :]).astype(
            jnp.float32
        ),
        axis=1,
    )
    row_weights = lax.dynamic_index_in_dim(counts_mat, group_id, 0, keepdims=False)
    col_weights = lax.dynamic_index_in_dim(counts_mat, group_id, 1, keepdims=False)
    channels = moment.shape[1]
    subs = 8
    width = channels // subs
    rows = jnp.stack([moment, feat_basis]).reshape(2, -1, subs, width)
    moment_part = split_sum(rows.transpose(2, 0, 1, 3).reshape(-1), index, sub_bits[::-1])
    moment_tab = tree_gather(moment_part, index, grp_bits).reshape(groups, 2, -1, width)
    mixed_part = jnp.einsum("j,jnkc->nkc", row_weights, moment_tab, precision=PRECISE)
    gathered_part = mixed_part[0]
    local_part = jnp.dot(trans_weight, gathered_part, precision=PRECISE)
    both = tree_gather(jnp.stack([local_part, mixed_part[1]]).reshape(-1), index, sub_bits)
    both = both.reshape(subs, 2, -1, width).transpose(1, 2, 0, 3).reshape(2, -1, channels)
    local_exp, feat_mixed = both[0], both[1]
    potential = jnp.einsum("ka,kc->ac", basis_val, local_exp, precision=PRECISE)
    pre_act = near_val + potential
    sigma = jax.nn.sigmoid(pre_act)
    activ = pre_act * sigma
    atom_energy = mask_f * jnp.dot(activ, read_weight, precision=PRECISE)
    d_pre = mask_f[:, None] * read_weight[None, :] * (sigma + pre_act * sigma * (1.0 - sigma))
    grad_read_part = jnp.dot(mask_f, activ, precision=PRECISE)
    d_local = jnp.dot(basis_val, d_pre, precision=PRECISE)
    d_basis = jnp.einsum("kc,ac->ka", local_exp, d_pre, precision=PRECISE)
    d_rows = d_local.reshape(-1, subs, width).transpose(1, 0, 2).reshape(-1)
    d_local_part = split_sum(d_rows, index, sub_bits[::-1]).reshape(-1, width)
    grad_trans_part = jnp.einsum("kc,qc->kq", d_local_part, gathered_part, precision=PRECISE)
    d_gathered_part = jnp.dot(trans_weight.T, d_local_part, precision=PRECISE)
    slice_width = d_gathered_part.shape[1]
    far_msg_part = jnp.einsum("ki,kc->ic", feat_mixed, d_gathered_part, precision=PRECISE)
    far_msg = lax.dynamic_update_slice_in_dim(
        jnp.zeros((far_msg_part.shape[0], slice_width * 8), jnp.float32),
        far_msg_part,
        (index % 8) * slice_width,
        axis=1,
    )
    d_own, d_ext, d_feat_ext = near_back(d_pre)
    d_pack = jnp.concatenate([d_ext, d_feat_ext], axis=0)
    low_pack = passed_along(d_pack[:, :atom_num].astype(jnp.bfloat16), "box", -1).astype(
        jnp.float32
    )
    high_pack = passed_along(d_pack[:, 2 * atom_num :].astype(jnp.bfloat16), "box", 1).astype(
        jnp.float32
    )
    low_pos, low_feat = low_pack[:3], low_pack[3:]
    high_pos, high_feat = high_pack[:3], high_pack[3:]
    d_hidden_near = d_feat_ext[:, atom_num : 2 * atom_num] + low_feat + high_feat
    grad_msg_part = (
        jnp.einsum("ai,ca->ic", masked_feat, d_hidden_near, precision=PRECISE) + far_msg
    )
    flat = jnp.concatenate(
        [grad_msg_part.reshape(-1), grad_trans_part.reshape(-1), grad_read_part.reshape(-1)]
    )
    d_tab, flat = tree_gather_sum(d_gathered_part.reshape(-1), flat, index, grp_bits)
    d_tab = d_tab.reshape(groups, -1, width)
    d_moment_part = jnp.einsum("b,bkc->kc", col_weights, d_tab, precision=PRECISE)
    d_moment, flat = tree_gather_sum(d_moment_part.reshape(-1), flat, index, sub_bits)
    d_moment = d_moment.reshape(subs, -1, width).transpose(1, 0, 2).reshape(-1, channels)
    d_basis = d_basis + jnp.dot(d_moment, hidden_t, precision=PRECISE)
    (d_far_pos,) = basis_back(d_basis)
    msg_size, trans_size = grad_msg_part.size, grad_trans_part.size
    grad_msg = flat[:msg_size].reshape(grad_msg_part.shape)
    grad_trans = flat[msg_size : msg_size + trans_size].reshape(grad_trans_part.shape)
    grad_read = flat[msg_size + trans_size :]
    forces = -(d_own + d_ext[:, atom_num : 2 * atom_num] + low_pos + high_pos + d_far_pos)
    return (atom_energy, forces, grad_msg, grad_trans, grad_read)


def solution(mesh):
    return jax.shard_map(
        on_device,
        mesh=mesh,
        in_specs=(
            P(None, "box"),
            P(None, "box"),
            P("box"),
            P("box", None),
            P(),
            P(),
            P(),
            P("box"),
            P("box"),
            P("box"),
            P(),
        ),
        out_specs=(P("box"), P(None, "box"), P(), P(), P()),
        check_vma=False,
    )
```
